256 devices in a mesh: ctx: 16 (over x, y_hi, core), tp: 16 (over z, y_lo).
Axes of the slice: x: 4, y: 4 (y_hi: 2, y_lo: 2; y = y_hi * 2 + y_lo), z: 8, core: 2. Of those that a mesh axis runs over, the one named last changes fastest.
Arguments:
- tokens: bfloat16 [2048, 4096], P('ctx', 'tp'), may hold values from -6 to 6
- gate_tiles: bfloat16 [1024, 128, 128], P('tp'), may hold values from -0.25 to 0.25
- up_tiles: bfloat16 [1024, 128, 128], P('tp'), may hold values from -0.25 to 0.25
- down_tiles: bfloat16 [1024, 128, 128], P('tp'), may hold values from -0.125 to 0.125
- gu_blocks: int32 [2, 1024], P(None, 'tp'), may hold values from 0 to 31, as said below
- down_blocks: int32 [2, 1024], P(None, 'tp'), may hold values from 0 to 31, as said below
- counts: int32 [2, 16], P(None, 'tp'), may hold values from 1 to 64, as said below
Outputs:
- mixed: bfloat16 [128, 16, 4096], P('tp', None, 'ctx')
The draws below stay inside these ranges and needn't reach their ends.
Inputs may be any that keep to these rules, and one draw needn't show every extreme that they name: `gu_blocks`: within one shard's 64 slots the pairs (row 0, row 1) are all different; row 0 is below 32, row 1 below 8. `down_blocks`: within one shard's 64 slots the pairs (row 0, row 1) are all different; row 0 is below 8, row 1 below 32. In each row some shard has exactly 64 live slots; only the first counts slots of a shard are live.
All inputs are finite; a program needn't handle non-finite values.
Results may differ from the reference program's by a relative error of at most 0.0052.
Values may be sent and summed in bfloat16 or wider, within the bound.
No kernel may reach another device: no remote copies, remote signals or barrier semaphores. Data moves between devices by JAX's collectives and lax.ppermute only.
A program may use at most 64 MiB of HBM per device.

```python
import jax
import jax.numpy as jnp
from jax import lax

D = 4096
BLK = 128
TOK_DEV = 128
IBLK = 32
HBLK = 8
MAXB = 64
TILES = 1024
TOKENS = 2048
SHARDS = 16
N_TP = 16


def draw_pattern(key, first_count, second_count):
    shard_count = TILES // MAXB
    shard_keys = jax.random.split(key, shard_count)

    def one_shard(shard_key):
        order = jax.random.permutation(shard_key, first_count * second_count)[:MAXB]
        return jnp.stack([order // second_count, order % second_count])
    both = jax.vmap(one_shard)(shard_keys)
    return jnp.transpose(both, (1, 0, 2)).reshape(2, TILES).astype(jnp.int32)


def draw_gu_blocks(key, part):
    return draw_pattern(jax.random.fold_in(key, 11), IBLK, HBLK)


def draw_down_blocks(key, part):
    return draw_pattern(jax.random.fold_in(key, 13), HBLK, IBLK)


def draw_counts(key, part):
    shard_count = TILES // MAXB
    base = jax.random.randint(jax.random.fold_in(key, 21), (2, shard_count), 1, MAXB + 1)
    busiest = jax.random.randint(jax.random.fold_in(key, 22), (2, 1), 0, shard_count)
    filled = jnp.where(jnp.arange(shard_count)[None, :] == busiest, MAXB, base)
    return filled.astype(jnp.int32)


def level_of(key, dims, cuts, least, largest):
    gain = 1.0
    for position, parts in cuts:
        heights = jax.random.uniform(jax.random.fold_in(jax.random.fold_in(key, 6), position), (parts,), jnp.float32, least / len(cuts), largest / len(cuts))
        gain = gain * jnp.repeat(jnp.exp(heights), dims[position] // parts).reshape((-1,) + (1,) * (len(dims) - 1 - position))
    return gain


def bell_draw(rng, extent, spread, reach, cuts=(), kind=jnp.bfloat16):
    array = jax.random.normal(rng, extent, jnp.float32) * spread
    if len(cuts) > 0:
        array = level_of(rng, extent, cuts, -0.22, 0.18) * array
    return jnp.clip(array, min=-reach, max=reach).astype(kind)


def setup_inputs(seed: int = 0) -> dict:
    key_list = jax.random.split(jax.random.key(seed), 8)
    return {
        "tokens": bell_draw(key_list[0], (TOKENS, D), 1.0, 6.0, ((0, 16), (1, 16))),
        "gate_tiles": bell_draw(key_list[1], (TILES, BLK, BLK), (MAXB * BLK // (2 * HBLK)) ** -0.5, 0.25, ((0, 16),)),
        "up_tiles": bell_draw(key_list[2], (TILES, BLK, BLK), (MAXB * BLK // (2 * HBLK)) ** -0.5, 0.25, ((0, 16),)),
        "down_tiles": bell_draw(key_list[3], (TILES, BLK, BLK), (N_TP * MAXB * BLK // (2 * IBLK)) ** -0.5, 0.125, ((0, 16),)),
        "gu_blocks": draw_gu_blocks(jax.random.fold_in(key_list[7], 71), 0),
        "down_blocks": draw_down_blocks(jax.random.fold_in(key_list[7], 71), 0),
        "counts": draw_counts(jax.random.fold_in(key_list[7], 71), 0),
    }


def shard_term(normed, gate_t, up_t, down_t, gu_b, dn_b, tile_counts):
    slot_ids = jnp.arange(MAXB)
    valid_in = (slot_ids < tile_counts[0]).astype(jnp.float32)
    valid_out = (slot_ids < tile_counts[1]).astype(jnp.float32)
    pick_hidden = (gu_b[1][:, None] == jnp.arange(HBLK)[None, :]).astype(jnp.float32) * valid_in[:, None]
    pick_out = (dn_b[1][:, None] == jnp.arange(IBLK)[None, :]).astype(jnp.float32) * valid_out[:, None]
    row_tiles = normed.reshape(TOKENS, IBLK, BLK)
    chosen = jnp.take(row_tiles, gu_b[0], axis=1).astype(jnp.float32)
    gate_part = jnp.einsum('tmk,mkn->tmn', chosen, gate_t.astype(jnp.float32))
    up_part = jnp.einsum('tmk,mkn->tmn', chosen, up_t.astype(jnp.float32))
    gate_sum = jnp.einsum('tmn,mh->thn', gate_part, pick_hidden, precision=lax.Precision.HIGHEST)
    up_sum = jnp.einsum('tmn,mh->thn', up_part, pick_hidden, precision=lax.Precision.HIGHEST)
    hidden = (jax.nn.silu(gate_sum) * up_sum).astype(jnp.bfloat16)
    chosen_hidden = jnp.take(hidden, dn_b[0], axis=1).astype(jnp.float32)
    products = jnp.einsum('tmk,mkn->tmn', chosen_hidden, down_t.astype(jnp.float32))
    summed = jnp.einsum('tmn,mo->ton', products, pick_out, precision=lax.Precision.HIGHEST)
    return summed.reshape(TOKENS, D)

def reference(tokens, gate_tiles, up_tiles, down_tiles, gu_blocks, down_blocks, counts):
    widened = tokens.astype(jnp.float32)
    squares = lax.optimization_barrier(jnp.mean(widened * widened, axis=1, keepdims=True))
    normed = (widened * lax.rsqrt(squares + 1e-05)).astype(jnp.bfloat16)

    def add_shard(shard_index, running):
        shard_index = jnp.asarray(shard_index).astype(jnp.int32)
        first_slot = (shard_index * MAXB).astype(jnp.int32)
        gate_t = lax.dynamic_slice_in_dim(gate_tiles, first_slot, MAXB, 0)
        up_t = lax.dynamic_slice_in_dim(up_tiles, first_slot, MAXB, 0)
        down_t = lax.dynamic_slice_in_dim(down_tiles, first_slot, MAXB, 0)
        gu_b = lax.dynamic_slice_in_dim(gu_blocks, first_slot, MAXB, 1)
        dn_b = lax.dynamic_slice_in_dim(down_blocks, first_slot, MAXB, 1)
        tile_counts = lax.dynamic_slice_in_dim(counts, shard_index, 1, 1)[:, 0]
        return running + shard_term(normed, gate_t, up_t, down_t, gu_b, dn_b, tile_counts)
    running = lax.fori_loop(0, N_TP, add_shard, jnp.zeros((TOKENS, D), jnp.float32))
    mixed = (widened + running).astype(jnp.bfloat16)
    return jnp.transpose(mixed.reshape(SHARDS, TOK_DEV, D), (1, 0, 2))
```

```python
import jax
import jax.numpy as jnp
from jax import lax
from jax.sharding import PartitionSpec as P

FF = 16384


def per_device(tokens, gate_tiles, up_tiles, down_tiles, gu_blocks, down_blocks, counts):
    tp_count = lax.axis_size("tp")
    ctx_count = lax.axis_size("ctx")
    own_rows, own_width = tokens.shape
    copies = jnp.broadcast_to(tokens[None], (tp_count, own_rows, own_width))
    pieces = lax.all_to_all(copies, "tp", 0, 0, tiled=True)
    gathered = jnp.transpose(pieces, (1, 0, 2)).reshape(own_rows, tp_count * own_width)
    tok_rows, feat_width = gathered.shape
    slot_count = gate_tiles.shape[0]
    tile_size = gate_tiles.shape[1]
    in_blocks = feat_width // tile_size
    hid_blocks = FF // tp_count // tile_size
    widened = gathered.astype(jnp.float32)
    squares = jnp.mean(widened * widened, axis=1, keepdims=True)
    normed = (widened * lax.rsqrt(squares + 1e-05)).astype(jnp.bfloat16)
    slot_ids = jnp.arange(slot_count)
    valid_in = (slot_ids < counts[0, 0]).astype(jnp.float32)
    valid_out = (slot_ids < counts[1, 0]).astype(jnp.float32)
    pick_hidden = (gu_blocks[1][:, None] == jnp.arange(hid_blocks)[None, :]).astype(
        jnp.float32
    ) * valid_in[:, None]
    pick_out = (down_blocks[1][:, None] == jnp.arange(in_blocks)[None, :]).astype(
        jnp.float32
    ) * valid_out[:, None]
    block_rows = min(tok_rows, 512)

    def hidden_block(row_block):
        row_tiles = row_block.reshape(block_rows, in_blocks, tile_size)
        chosen = jnp.take(row_tiles, gu_blocks[0], axis=1)
        gate_part = jnp.einsum(
            "tmk,mkn->tmn", chosen, gate_tiles, preferred_element_type=jnp.float32
        )
        up_part = jnp.einsum("tmk,mkn->tmn", chosen, up_tiles, preferred_element_type=jnp.float32)
        gate_sum = jnp.einsum(
            "tmn,mh->thn", gate_part, pick_hidden, precision=lax.Precision.HIGHEST
        )
        up_sum = jnp.einsum("tmn,mh->thn", up_part, pick_hidden, precision=lax.Precision.HIGHEST)
        return (jax.nn.silu(gate_sum) * up_sum).astype(jnp.bfloat16)

    hidden = lax.map(hidden_block, normed.reshape(tok_rows // block_rows, block_rows, feat_width))
    hidden = hidden.reshape(tok_rows, hid_blocks, tile_size)
    chosen_hidden = jnp.take(hidden, down_blocks[0], axis=1)
    products = jnp.einsum(
        "tmk,mkn->tmn", chosen_hidden, down_tiles, preferred_element_type=jnp.float32
    )
    summed = jnp.einsum("tmn,mo->ton", products, pick_out, precision=lax.Precision.HIGHEST)
    share = tok_rows // tp_count
    outgoing = summed.reshape(tp_count, share, feat_width).astype(jnp.bfloat16)
    incoming = lax.all_to_all(outgoing, "tp", 0, 0, tiled=True)
    total = jnp.sum(incoming.astype(jnp.float32), axis=0)
    residual = lax.dynamic_slice_in_dim(widened, lax.axis_index("tp") * share, share, 0)
    mixed = (total + residual).astype(jnp.bfloat16)
    return lax.all_to_all(
        mixed.reshape(share, ctx_count, feat_width // ctx_count), "ctx", 1, 1, tiled=True
    )


def solution(mesh):
    return jax.shard_map(
        per_device,
        mesh=mesh,
        in_specs=(
            P("ctx", "tp"),
            P("tp", None, None),
            P("tp", None, None),
            P("tp", None, None),
            P(None, "tp"),
            P(None, "tp"),
            P(None, "tp"),
        ),
        out_specs=P("tp", None, "ctx"),
        check_vma=False,
    )
```

```python
import jax
import jax.numpy as jnp
from jax import lax
from jax.experimental import pallas as pl
from jax.experimental.pallas import tpu as pltpu
from jax.sharding import PartitionSpec as P

FF = 16384


def ffn_kernel(cnt_ref, gu_ref, dn_ref, pieces_ref, g_ref, u_ref, d_ref, out_ref,
               normed_s, accg_s, accu_s, hid_s, acco_s):
    n_src, rows, width = pieces_ref.shape
    tile = g_ref.shape[1]
    per_src = width // tile
    feat = n_src * width
    ss = jnp.zeros((rows, 1), jnp.float32)
    for s in range(n_src):
        x = pieces_ref[s].astype(jnp.float32)
        ss = ss + jnp.sum(x * x, axis=1, keepdims=True)
    scale = lax.rsqrt(ss / feat + 1e-05)
    for s in range(n_src):
        for h in range(per_src):
            x = pieces_ref[s, :, h * tile:(h + 1) * tile].astype(jnp.float32)
            normed_s[s * per_src + h] = (x * scale).astype(jnp.bfloat16)
    accg_s[...] = jnp.zeros(accg_s.shape, jnp.float32)
    accu_s[...] = jnp.zeros(accu_s.shape, jnp.float32)

    def gu_body(m, carry):
        x = normed_s[gu_ref[0, m]]
        h = gu_ref[1, m]
        accg_s[h] += jnp.dot(x, g_ref[m], preferred_element_type=jnp.float32)
        accu_s[h] += jnp.dot(x, u_ref[m], preferred_element_type=jnp.float32)
        return carry

    lax.fori_loop(0, cnt_ref[0], gu_body, 0)
    g = accg_s[...]
    hid_s[...] = (g / (1.0 + jnp.exp(-g)) * accu_s[...]).astype(jnp.bfloat16)
    acco_s[...] = jnp.zeros(acco_s.shape, jnp.float32)

    def dn_body(m, carry):
        o = dn_ref[1, m]
        acco_s[o] += jnp.dot(hid_s[dn_ref[0, m]], d_ref[m], preferred_element_type=jnp.float32)
        return carry

    lax.fori_loop(0, cnt_ref[1], dn_body, 0)
    out_ref[...] = acco_s[...].astype(out_ref.dtype)


def ffn(counts, gu_blocks, down_blocks, pieces, gate_tiles, up_tiles, down_tiles, hid_blocks, out_dtype):
    n_src, rows, width = pieces.shape
    tile = gate_tiles.shape[1]
    in_blocks = n_src * width // tile
    smem = pl.BlockSpec(memory_space=pltpu.SMEM)
    vmem = pl.BlockSpec(memory_space=pltpu.VMEM)
    return pl.pallas_call(
        ffn_kernel,
        out_shape=jax.ShapeDtypeStruct((in_blocks, rows, tile), out_dtype),
        in_specs=[smem, smem, smem, vmem, vmem, vmem, vmem],
        out_specs=vmem,
        scratch_shapes=[
            pltpu.VMEM((in_blocks, rows, tile), jnp.bfloat16),
            pltpu.VMEM((hid_blocks, rows, tile), jnp.float32),
            pltpu.VMEM((hid_blocks, rows, tile), jnp.float32),
            pltpu.VMEM((hid_blocks, rows, tile), jnp.bfloat16),
            pltpu.VMEM((in_blocks, rows, tile), jnp.float32),
        ],
    )(counts.reshape(-1), gu_blocks, down_blocks, pieces, gate_tiles, up_tiles, down_tiles)


def per_device(tokens, gate_tiles, up_tiles, down_tiles, gu_blocks, down_blocks, counts):
    tp_count = lax.axis_size("tp")
    ctx_count = lax.axis_size("ctx")
    own_rows, own_width = tokens.shape
    copies = jnp.broadcast_to(tokens[None], (tp_count, own_rows, own_width))
    pieces = lax.all_to_all(copies, "tp", 0, 0, tiled=True)
    tile = gate_tiles.shape[1]
    feat_width = tp_count * own_width
    in_blocks = feat_width // tile
    hid_blocks = FF // tp_count // tile
    partial = ffn(counts, gu_blocks, down_blocks, pieces, gate_tiles, up_tiles, down_tiles,
                  hid_blocks, jnp.bfloat16)
    share = own_rows // tp_count
    outgoing = partial.reshape(in_blocks, tp_count, share, tile).transpose(1, 2, 0, 3)
    incoming = lax.all_to_all(outgoing.reshape(tp_count, share, feat_width), "tp", 0, 0, tiled=True)
    total = jnp.sum(incoming.astype(jnp.float32), axis=0)
    own = lax.dynamic_slice_in_dim(pieces, lax.axis_index("tp") * share, share, 1)
    residual = jnp.transpose(own, (1, 0, 2)).reshape(share, feat_width).astype(jnp.float32)
    mixed = (total + residual).astype(jnp.bfloat16)
    return lax.all_to_all(
        mixed.reshape(share, ctx_count, feat_width // ctx_count), "ctx", 1, 1, tiled=True
    )


def solution(mesh):
    return jax.shard_map(
        per_device,
        mesh=mesh,
        in_specs=(
            P("ctx", "tp"),
            P("tp", None, None),
            P("tp", None, None),
            P("tp", None, None),
            P(None, "tp"),
            P(None, "tp"),
            P(None, "tp"),
        ),
        out_specs=P("tp", None, "ctx"),
        check_vma=False,
    )
```

```python
import jax
import jax.numpy as jnp
from jax import lax
from jax.experimental import pallas as pl
from jax.experimental.pallas import tpu as pltpu
from jax.sharding import PartitionSpec as P

FF = 16384
Y_LO = 2


def ffn_kernel(cnt_ref, gu_ref, dn_ref, pieces_ref, g_ref, u_ref, d_ref, out_ref,
               normed_s, accg_s, accu_s, hid_s, acco_s):
    n_src, rows, width = pieces_ref.shape
    tile = g_ref.shape[1]
    per_src = width // tile
    feat = n_src * width
    ss = jnp.zeros((rows, 1), jnp.float32)
    for s in range(n_src):
        x = pieces_ref[s].astype(jnp.float32)
        ss = ss + jnp.sum(x * x, axis=1, keepdims=True)
    scale = lax.rsqrt(ss / feat + 1e-05)
    for s in range(n_src):
        for h in range(per_src):
            x = pieces_ref[s, :, h * tile:(h + 1) * tile].astype(jnp.float32)
            normed_s[s * per_src + h] = (x * scale).astype(jnp.bfloat16)
    accg_s[...] = jnp.zeros(accg_s.shape, jnp.float32)
    accu_s[...] = jnp.zeros(accu_s.shape, jnp.float32)

    def gu_body(m, carry):
        x = normed_s[gu_ref[0, m]]
        h = gu_ref[1, m]
        accg_s[h] += jnp.dot(x, g_ref[m], preferred_element_type=jnp.float32)
        accu_s[h] += jnp.dot(x, u_ref[m], preferred_element_type=jnp.float32)
        return carry

    lax.fori_loop(0, cnt_ref[0], gu_body, 0)
    g = accg_s[...]
    hid_s[...] = (g / (1.0 + jnp.exp(-g)) * accu_s[...]).astype(jnp.bfloat16)
    acco_s[...] = jnp.zeros(acco_s.shape, jnp.float32)

    def dn_body(m, carry):
        o = dn_ref[1, m]
        acco_s[o] += jnp.dot(hid_s[dn_ref[0, m]], d_ref[m], preferred_element_type=jnp.float32)
        return carry

    lax.fori_loop(0, cnt_ref[1], dn_body, 0)
    out_ref[...] = acco_s[...].astype(out_ref.dtype)


def ffn(counts, gu_blocks, down_blocks, pieces, gate_tiles, up_tiles, down_tiles, hid_blocks, out_dtype):
    n_src, rows, width = pieces.shape
    tile = gate_tiles.shape[1]
    in_blocks = n_src * width // tile
    smem = pl.BlockSpec(memory_space=pltpu.SMEM)
    vmem = pl.BlockSpec(memory_space=pltpu.VMEM)
    return pl.pallas_call(
        ffn_kernel,
        out_shape=jax.ShapeDtypeStruct((in_blocks, rows, tile), out_dtype),
        in_specs=[smem, smem, smem, vmem, vmem, vmem, vmem],
        out_specs=vmem,
        scratch_shapes=[
            pltpu.VMEM((in_blocks, rows, tile), jnp.bfloat16),
            pltpu.VMEM((hid_blocks, rows, tile), jnp.float32),
            pltpu.VMEM((hid_blocks, rows, tile), jnp.float32),
            pltpu.VMEM((hid_blocks, rows, tile), jnp.bfloat16),
            pltpu.VMEM((in_blocks, rows, tile), jnp.float32),
        ],
    )(counts.reshape(-1), gu_blocks, down_blocks, pieces, gate_tiles, up_tiles, down_tiles)


def ring_pairs(count, step):
    return [(i, ((i // Y_LO + step) % count) * Y_LO + i % Y_LO) for i in range(count * Y_LO)]


def per_device(tokens, gate_tiles, up_tiles, down_tiles, gu_blocks, down_blocks, counts):
    tp_count = lax.axis_size("tp")
    ctx_count = lax.axis_size("ctx")
    z_count = tp_count // Y_LO
    own_rows, own_width = tokens.shape
    tile = gate_tiles.shape[1]
    per_src = own_width // tile
    me = lax.axis_index("tp")
    my_z = me // Y_LO
    my_y = me % Y_LO
    partner = lax.ppermute(tokens, "tp", [(i, i ^ 1) for i in range(tp_count)])
    both = jnp.where(my_y == 0, jnp.stack([tokens, partner]), jnp.stack([partner, tokens]))
    ahead, behind = [], []
    fwd = bwd = both
    for k in range(1, z_count // 2 + 1):
        fwd = lax.ppermute(fwd, "tp", ring_pairs(z_count, 1))
        ahead.append(fwd)
        if k < z_count - z_count // 2:
            bwd = lax.ppermute(bwd, "tp", ring_pairs(z_count, -1))
            behind.append(bwd)
    pieces = jnp.concatenate([both] + ahead + behind)
    src_ids = jnp.arange(tp_count)
    dz = (src_ids // Y_LO - my_z) % z_count
    slot_of_z = jnp.where(dz == 0, 0, jnp.where(dz >= z_count // 2, z_count - dz, z_count // 2 + dz))
    position = slot_of_z * Y_LO + src_ids % Y_LO
    in_tile = gu_blocks[0]
    moved = position[in_tile // per_src] * per_src + in_tile % per_src
    gu_local = jnp.stack([moved, gu_blocks[1]])
    feat_width = tp_count * own_width
    in_blocks = feat_width // tile
    hid_blocks = FF // tp_count // tile
    partial = ffn(counts, gu_local, down_blocks, pieces, gate_tiles, up_tiles, down_tiles,
                  hid_blocks, jnp.bfloat16)
    share = own_rows // tp_count
    outgoing = partial.reshape(in_blocks, tp_count, share, tile).transpose(1, 2, 0, 3)
    incoming = lax.all_to_all(outgoing.reshape(tp_count, share, feat_width), "tp", 0, 0, tiled=True)
    total = jnp.sum(incoming.astype(jnp.float32), axis=0)
    own = jnp.take(lax.dynamic_slice_in_dim(pieces, me * share, share, 1), position, axis=0)
    residual = jnp.transpose(own, (1, 0, 2)).reshape(share, feat_width).astype(jnp.float32)
    mixed = (total + residual).astype(jnp.bfloat16)
    return lax.all_to_all(
        mixed.reshape(share, ctx_count, feat_width // ctx_count), "ctx", 1, 1, tiled=True
    )

def solution(mesh):
    return jax.shard_map(
        per_device,
        mesh=mesh,
        in_specs=(
            P("ctx", "tp"),
            P("tp", None, None),
            P("tp", None, None),
            P("tp", None, None),
            P(None, "tp"),
            P(None, "tp"),
            P(None, "tp"),
        ),
        out_specs=P("tp", None, "ctx"),
        check_vma=False,
    )
```

```python
import jax
import jax.numpy as jnp
from jax import lax
from jax.experimental import pallas as pl
from jax.experimental.pallas import tpu as pltpu
from jax.sharding import PartitionSpec as P

FF = 16384
Y_LO = 2


def ffn_kernel(cnt_ref, gu_ref, dn_ref, pieces_ref, g_ref, u_ref, d_ref, out_ref,
               normed_s, accg_s, accu_s, hid_s, acco_s):
    n_src, rows, width = pieces_ref.shape
    tile = g_ref.shape[1]
    per_src = width // tile
    feat = n_src * width
    ss = jnp.zeros((rows, 1), jnp.float32)
    for s in range(n_src):
        x = pieces_ref[s].astype(jnp.float32)
        ss = ss + jnp.sum(x * x, axis=1, keepdims=True)
    scale = lax.rsqrt(ss / feat + 1e-05)
    for s in range(n_src):
        for h in range(per_src):
            x = pieces_ref[s, :, h * tile:(h + 1) * tile].astype(jnp.float32)
            normed_s[s * per_src + h] = (x * scale).astype(jnp.bfloat16)
    accg_s[...] = jnp.zeros(accg_s.shape, jnp.float32)
    accu_s[...] = jnp.zeros(accu_s.shape, jnp.float32)

    def gu_body(m, carry):
        x = normed_s[gu_ref[0, m]]
        h = gu_ref[1, m]
        accg_s[h] += jnp.dot(x, g_ref[m], preferred_element_type=jnp.float32)
        accu_s[h] += jnp.dot(x, u_ref[m], preferred_element_type=jnp.float32)
        return carry

    lax.fori_loop(0, cnt_ref[0], gu_body, 0)
    g = accg_s[...]
    hid_s[...] = (g / (1.0 + jnp.exp(-g)) * accu_s[...]).astype(jnp.bfloat16)
    acco_s[...] = jnp.zeros(acco_s.shape, jnp.float32)

    def dn_body(m, carry):
        o = dn_ref[1, m]
        acco_s[o] += jnp.dot(hid_s[dn_ref[0, m]], d_ref[m], preferred_element_type=jnp.float32)
        return carry

    lax.fori_loop(0, cnt_ref[1], dn_body, 0)
    out_ref[...] = acco_s[...].astype(out_ref.dtype)


def ffn(counts, gu_blocks, down_blocks, pieces, gate_tiles, up_tiles, down_tiles, hid_blocks, out_dtype):
    n_src, rows, width = pieces.shape
    tile = gate_tiles.shape[1]
    in_blocks = n_src * width // tile
    smem = pl.BlockSpec(memory_space=pltpu.SMEM)
    vmem = pl.BlockSpec(memory_space=pltpu.VMEM)
    return pl.pallas_call(
        ffn_kernel,
        out_shape=jax.ShapeDtypeStruct((in_blocks, rows, tile), out_dtype),
        in_specs=[smem, smem, smem, vmem, vmem, vmem, vmem],
        out_specs=vmem,
        scratch_shapes=[
            pltpu.VMEM((in_blocks, rows, tile), jnp.bfloat16),
            pltpu.VMEM((hid_blocks, rows, tile), jnp.float32),
            pltpu.VMEM((hid_blocks, rows, tile), jnp.float32),
            pltpu.VMEM((hid_blocks, rows, tile), jnp.bfloat16),
            pltpu.VMEM((in_blocks, rows, tile), jnp.float32),
        ],
    )(counts.reshape(-1), gu_blocks, down_blocks, pieces, gate_tiles, up_tiles, down_tiles)


def ring_pairs(count, step):
    return [(i, ((i // Y_LO + step) % count) * Y_LO + i % Y_LO) for i in range(count * Y_LO)]


def per_device(tokens, gate_tiles, up_tiles, down_tiles, gu_blocks, down_blocks, counts):
    tp_count = lax.axis_size("tp")
    ctx_count = lax.axis_size("ctx")
    z_count = tp_count // Y_LO
    own_rows, own_width = tokens.shape
    tile = gate_tiles.shape[1]
    per_src = own_width // tile
    me = lax.axis_index("tp")
    my_z = me // Y_LO
    my_y = me % Y_LO
    def shifted(piece, dz, flip):
        return lax.ppermute(piece, "tp", [
            (i, ((i // Y_LO + dz) % z_count) * Y_LO + (i % Y_LO ^ flip)) for i in range(tp_count)
        ])

    def ordered(mine, other):
        return jnp.where(my_y == 0, jnp.stack([mine, other]), jnp.stack([other, mine]))

    both = ordered(tokens, shifted(tokens, 0, 1))
    fwd = ordered(shifted(tokens, 1, 0), shifted(tokens, 1, 1))
    bwd = ordered(shifted(tokens, -1, 0), shifted(tokens, -1, 1))
    ahead, behind = [fwd], [bwd]
    for k in range(2, z_count // 2 + 1):
        fwd = lax.ppermute(fwd, "tp", ring_pairs(z_count, 1))
        ahead.append(fwd)
        if k < z_count - z_count // 2:
            bwd = lax.ppermute(bwd, "tp", ring_pairs(z_count, -1))
            behind.append(bwd)
    pieces = jnp.concatenate([both] + ahead + behind)
    src_ids = jnp.arange(tp_count)
    dz = (src_ids // Y_LO - my_z) % z_count
    slot_of_z = jnp.where(dz == 0, 0, jnp.where(dz >= z_count // 2, z_count - dz, z_count // 2 + dz))
    position = slot_of_z * Y_LO + src_ids % Y_LO
    in_tile = gu_blocks[0]
    moved = position[in_tile // per_src] * per_src + in_tile % per_src
    gu_local = jnp.stack([moved, gu_blocks[1]])
    feat_width = tp_count * own_width
    in_blocks = feat_width // tile
    hid_blocks = FF // tp_count // tile
    partial = ffn(counts, gu_local, down_blocks, pieces, gate_tiles, up_tiles, down_tiles,
                  hid_blocks, jnp.bfloat16)
    share = own_rows // tp_count
    outgoing = partial.reshape(in_blocks, tp_count, share, tile).transpose(1, 2, 0, 3)
    incoming = lax.all_to_all(outgoing.reshape(tp_count, share, feat_width), "tp", 0, 0, tiled=True)
    total = jnp.sum(incoming.astype(jnp.float32), axis=0)
    own = jnp.take(lax.dynamic_slice_in_dim(pieces, me * share, share, 1), position, axis=0)
    residual = jnp.transpose(own, (1, 0, 2)).reshape(share, feat_width).astype(jnp.float32)
    mixed = (total + residual).astype(jnp.bfloat16)
    return lax.all_to_all(
        mixed.reshape(share, ctx_count, feat_width // ctx_count), "ctx", 1, 1, tiled=True
    )

def solution(mesh):
    return jax.shard_map(
        per_device,
        mesh=mesh,
        in_specs=(
            P("ctx", "tp"),
            P("tp", None, None),
            P("tp", None, None),
            P("tp", None, None),
            P(None, "tp"),
            P(None, "tp"),
            P(None, "tp"),
        ),
        out_specs=P("tp", None, "ctx"),
        check_vma=False,
    )
```

```python
import jax
import jax.numpy as jnp
from jax import lax
from jax.experimental import pallas as pl
from jax.experimental.pallas import tpu as pltpu
from jax.sharding import PartitionSpec as P

FF = 16384
Y_LO = 2
UNROLL = 8


def ffn_kernel(cnt_ref, gu_ref, dn_ref, pieces_ref, g_ref, u_ref, d_ref, out_ref,
               normed_s, accg_s, accu_s, hid_s, acco_s):
    n_src, rows, width = pieces_ref.shape
    tile = g_ref.shape[1]
    per_src = width // tile
    feat = n_src * width
    ss = jnp.zeros((rows, 1), jnp.float32)
    for s in range(n_src):
        x = pieces_ref[s].astype(jnp.float32)
        ss = ss + jnp.sum(x * x, axis=1, keepdims=True)
    scale = lax.rsqrt(ss / feat + 1e-05)
    for s in range(n_src):
        for h in range(per_src):
            x = pieces_ref[s, :, h * tile:(h + 1) * tile].astype(jnp.float32)
            normed_s[s * per_src + h] = (x * scale).astype(jnp.bfloat16)
    accg_s[...] = jnp.zeros(accg_s.shape, jnp.float32)
    accu_s[...] = jnp.zeros(accu_s.shape, jnp.float32)

    def gu_body(m, carry):
        x = normed_s[gu_ref[0, m]]
        h = gu_ref[1, m]
        live = (m < cnt_ref[0]).astype(jnp.float32)
        accg_s[h] += jnp.dot(x, g_ref[m], preferred_element_type=jnp.float32) * live
        accu_s[h] += jnp.dot(x, u_ref[m], preferred_element_type=jnp.float32) * live
        return carry

    lax.fori_loop(0, g_ref.shape[0], gu_body, 0, unroll=UNROLL)
    g = accg_s[...]
    hid_s[...] = (g / (1.0 + jnp.exp(-g)) * accu_s[...]).astype(jnp.bfloat16)
    acco_s[...] = jnp.zeros(acco_s.shape, jnp.float32)

    def dn_body(m, carry):
        o = dn_ref[1, m]
        live = (m < cnt_ref[1]).astype(jnp.float32)
        acco_s[o] += jnp.dot(hid_s[dn_ref[0, m]], d_ref[m], preferred_element_type=jnp.float32) * live
        return carry

    lax.fori_loop(0, d_ref.shape[0], dn_body, 0, unroll=UNROLL)
    out_ref[...] = acco_s[...].astype(out_ref.dtype)


def ffn(counts, gu_blocks, down_blocks, pieces, gate_tiles, up_tiles, down_tiles, hid_blocks, out_dtype):
    n_src, rows, width = pieces.shape
    tile = gate_tiles.shape[1]
    in_blocks = n_src * width // tile
    smem = pl.BlockSpec(memory_space=pltpu.SMEM)
    vmem = pl.BlockSpec(memory_space=pltpu.VMEM)
    return pl.pallas_call(
        ffn_kernel,
        out_shape=jax.ShapeDtypeStruct((in_blocks, rows, tile), out_dtype),
        in_specs=[smem, smem, smem, vmem, vmem, vmem, vmem],
        out_specs=vmem,
        scratch_shapes=[
            pltpu.VMEM((in_blocks, rows, tile), jnp.bfloat16),
            pltpu.VMEM((hid_blocks, rows, tile), jnp.float32),
            pltpu.VMEM((hid_blocks, rows, tile), jnp.float32),
            pltpu.VMEM((hid_blocks, rows, tile), jnp.bfloat16),
            pltpu.VMEM((in_blocks, rows, tile), jnp.float32),
        ],
    )(counts.reshape(-1), gu_blocks, down_blocks, pieces, gate_tiles, up_tiles, down_tiles)


def ring_pairs(count, step):
    return [(i, ((i // Y_LO + step) % count) * Y_LO + i % Y_LO) for i in range(count * Y_LO)]


def per_device(tokens, gate_tiles, up_tiles, down_tiles, gu_blocks, down_blocks, counts):
    tp_count = lax.axis_size("tp")
    ctx_count = lax.axis_size("ctx")
    z_count = tp_count // Y_LO
    own_rows, own_width = tokens.shape
    tile = gate_tiles.shape[1]
    per_src = own_width // tile
    me = lax.axis_index("tp")
    my_z = me // Y_LO
    my_y = me % Y_LO
    partner = lax.ppermute(tokens, "tp", [(i, i ^ 1) for i in range(tp_count)])
    both = jnp.where(my_y == 0, jnp.stack([tokens, partner]), jnp.stack([partner, tokens]))
    ahead, behind = [], []
    fwd = bwd = both
    for k in range(1, z_count // 2 + 1):
        fwd = lax.ppermute(fwd, "tp", ring_pairs(z_count, 1))
        ahead.append(fwd)
        if k < z_count - z_count // 2:
            bwd = lax.ppermute(bwd, "tp", ring_pairs(z_count, -1))
            behind.append(bwd)
    pieces = jnp.concatenate([both] + ahead + behind)
    src_ids = jnp.arange(tp_count)
    dz = (src_ids // Y_LO - my_z) % z_count
    slot_of_z = jnp.where(dz == 0, 0, jnp.where(dz >= z_count // 2, z_count - dz, z_count // 2 + dz))
    position = slot_of_z * Y_LO + src_ids % Y_LO
    in_tile = gu_blocks[0]
    moved = position[in_tile // per_src] * per_src + in_tile % per_src
    gu_local = jnp.stack([moved, gu_blocks[1]])
    feat_width = tp_count * own_width
    in_blocks = feat_width // tile
    hid_blocks = FF // tp_count // tile
    partial = ffn(counts, gu_local, down_blocks, pieces, gate_tiles, up_tiles, down_tiles,
                  hid_blocks, jnp.bfloat16)
    share = own_rows // tp_count
    outgoing = partial.reshape(in_blocks, tp_count, share, tile).transpose(1, 2, 0, 3)
    incoming = lax.all_to_all(outgoing.reshape(tp_count, share, feat_width), "tp", 0, 0, tiled=True)
    total = jnp.sum(incoming.astype(jnp.float32), axis=0)
    own = jnp.take(lax.dynamic_slice_in_dim(pieces, me * share, share, 1), position, axis=0)
    residual = jnp.transpose(own, (1, 0, 2)).reshape(share, feat_width).astype(jnp.float32)
    mixed = (total + residual).astype(jnp.bfloat16)
    return lax.all_to_all(
        mixed.reshape(share, ctx_count, feat_width // ctx_count), "ctx", 1, 1, tiled=True
    )

def solution(mesh):
    return jax.shard_map(
        per_device,
        mesh=mesh,
        in_specs=(
            P("ctx", "tp"),
            P("tp", None, None),
            P("tp", None, None),
            P("tp", None, None),
            P(None, "tp"),
            P(None, "tp"),
            P(None, "tp"),
        ),
        out_specs=P("tp", None, "ctx"),
        check_vma=False,
    )
```

```python
import jax
import jax.numpy as jnp
from jax import lax
from jax.experimental import pallas as pl
from jax.experimental.pallas import tpu as pltpu
from jax.sharding import PartitionSpec as P

FF = 16384
Y_LO = 2
UNROLL = 8


def ffn_kernel(cnt_ref, gu_ref, dn_ref, me_ref, pieces_ref, g_ref, u_ref, d_ref, res_ref, out_ref,
               normed_s, accg_s, accu_s, hid_s, acco_s):
    n_src, rows, width = pieces_ref.shape
    tile = g_ref.shape[1]
    per_src = width // tile
    feat = n_src * width
    ss = jnp.zeros((rows, 1), jnp.float32)
    for s in range(n_src):
        x = pieces_ref[s].astype(jnp.float32)
        ss = ss + jnp.sum(x * x, axis=1, keepdims=True)
    scale = lax.rsqrt(ss / feat + 1e-05)
    for s in range(n_src):
        for h in range(per_src):
            x = pieces_ref[s, :, h * tile:(h + 1) * tile].astype(jnp.float32)
            normed_s[s * per_src + h] = (x * scale).astype(jnp.bfloat16)
    accg_s[...] = jnp.zeros(accg_s.shape, jnp.float32)
    accu_s[...] = jnp.zeros(accu_s.shape, jnp.float32)

    def gu_body(m, carry):
        x = normed_s[gu_ref[0, m]]
        h = gu_ref[1, m]
        live = (m < cnt_ref[0]).astype(jnp.float32)
        accg_s[h] += jnp.dot(x, g_ref[m], preferred_element_type=jnp.float32) * live
        accu_s[h] += jnp.dot(x, u_ref[m], preferred_element_type=jnp.float32) * live
        return carry

    lax.fori_loop(0, g_ref.shape[0], gu_body, 0, unroll=UNROLL)
    g = accg_s[...]
    hid_s[...] = (g / (1.0 + jnp.exp(-g)) * accu_s[...]).astype(jnp.bfloat16)
    acco_s[...] = jnp.zeros(acco_s.shape, jnp.float32)

    def dn_body(m, carry):
        o = dn_ref[1, m]
        live = (m < cnt_ref[1]).astype(jnp.float32)
        acco_s[o] += jnp.dot(hid_s[dn_ref[0, m]], d_ref[m], preferred_element_type=jnp.float32) * live
        return carry

    lax.fori_loop(0, d_ref.shape[0], dn_body, 0, unroll=UNROLL)
    groups, dests, share, group_width = out_ref.shape
    rows = pl.ds(pl.multiple_of(me_ref[0] * share, share), share)
    per_group = group_width // tile
    for o in range(acco_s.shape[0]):
        acco_s[o, rows, :] += res_ref[:, o * tile:(o + 1) * tile]
        block = acco_s[o].reshape(dests, share, tile).astype(out_ref.dtype)
        group, half = divmod(o, per_group)
        out_ref[group, :, :, half * tile:(half + 1) * tile] = block


def ffn(counts, gu_blocks, down_blocks, me, pieces, gate_tiles, up_tiles, down_tiles, residual,
        hid_blocks, groups):
    n_src, rows, width = pieces.shape
    tile = gate_tiles.shape[1]
    in_blocks = n_src * width // tile
    share = residual.shape[0]
    smem = pl.BlockSpec(memory_space=pltpu.SMEM)
    vmem = pl.BlockSpec(memory_space=pltpu.VMEM)
    return pl.pallas_call(
        ffn_kernel,
        out_shape=jax.ShapeDtypeStruct((groups, rows // share, share, in_blocks * tile // groups),
                                       jnp.bfloat16),
        in_specs=[smem, smem, smem, smem, vmem, vmem, vmem, vmem, vmem],
        out_specs=vmem,
        scratch_shapes=[
            pltpu.VMEM((in_blocks, rows, tile), jnp.bfloat16),
            pltpu.VMEM((hid_blocks, rows, tile), jnp.float32),
            pltpu.VMEM((hid_blocks, rows, tile), jnp.float32),
            pltpu.VMEM((hid_blocks, rows, tile), jnp.bfloat16),
            pltpu.VMEM((in_blocks, rows, tile), jnp.float32),
        ],
    )(counts.reshape(-1), gu_blocks, down_blocks, me.reshape(1), pieces, gate_tiles, up_tiles,
      down_tiles, residual)

def ring_pairs(count, step):
    return [(i, ((i // Y_LO + step) % count) * Y_LO + i % Y_LO) for i in range(count * Y_LO)]


def per_device(tokens, gate_tiles, up_tiles, down_tiles, gu_blocks, down_blocks, counts):
    tp_count = lax.axis_size("tp")
    ctx_count = lax.axis_size("ctx")
    z_count = tp_count // Y_LO
    own_rows, own_width = tokens.shape
    tile = gate_tiles.shape[1]
    per_src = own_width // tile
    me = lax.axis_index("tp")
    my_z = me // Y_LO
    my_y = me % Y_LO
    partner = lax.ppermute(tokens, "tp", [(i, i ^ 1) for i in range(tp_count)])
    both = jnp.where(my_y == 0, jnp.stack([tokens, partner]), jnp.stack([partner, tokens]))
    ahead, behind = [], []
    fwd = bwd = both
    for k in range(1, z_count // 2 + 1):
        fwd = lax.ppermute(fwd, "tp", ring_pairs(z_count, 1))
        ahead.append(fwd)
        if k < z_count - z_count // 2:
            bwd = lax.ppermute(bwd, "tp", ring_pairs(z_count, -1))
            behind.append(bwd)
    pieces = jnp.concatenate([both] + ahead + behind)
    src_ids = jnp.arange(tp_count)
    dz = (src_ids // Y_LO - my_z) % z_count
    slot_of_z = jnp.where(dz == 0, 0, jnp.where(dz >= z_count // 2, z_count - dz, z_count // 2 + dz))
    position = slot_of_z * Y_LO + src_ids % Y_LO
    in_tile = gu_blocks[0]
    moved = position[in_tile // per_src] * per_src + in_tile % per_src
    gu_local = jnp.stack([moved, gu_blocks[1]])
    feat_width = tp_count * own_width
    in_blocks = feat_width // tile
    hid_blocks = FF // tp_count // tile
    share = own_rows // tp_count
    own = jnp.take(lax.dynamic_slice_in_dim(pieces, me * share, share, 1), position, axis=0)
    residual = jnp.transpose(own, (1, 0, 2)).reshape(share, feat_width).astype(jnp.float32)
    outgoing = ffn(counts, gu_local, down_blocks, me.astype(jnp.int32), pieces, gate_tiles,
                   up_tiles, down_tiles, residual, hid_blocks, ctx_count)
    incoming = lax.all_to_all(
        outgoing.reshape(ctx_count * tp_count, share, feat_width // ctx_count),
        ("ctx", "tp"), 0, 0, tiled=True,
    )
    total = jnp.sum(
        incoming.reshape(ctx_count, tp_count, share, -1).astype(jnp.float32), axis=1
    )
    return jnp.transpose(total, (1, 0, 2)).astype(jnp.bfloat16)

def solution(mesh):
    return jax.shard_map(
        per_device,
        mesh=mesh,
        in_specs=(
            P("ctx", "tp"),
            P("tp", None, None),
            P("tp", None, None),
            P("tp", None, None),
            P(None, "tp"),
            P(None, "tp"),
            P(None, "tp"),
        ),
        out_specs=P("tp", None, "ctx"),
        check_vma=False,
    )
```

```python
import jax
import jax.numpy as jnp
from jax import lax
from jax.experimental import pallas as pl
from jax.experimental.pallas import tpu as pltpu
from jax.sharding import PartitionSpec as P

FF = 16384
Y_LO = 2
UNROLL = 8


def ffn_kernel(cnt_ref, gu_ref, dn_ref, me_ref, pieces_ref, g_hbm, u_hbm, d_hbm, res_ref, out_ref,
               normed_s, accg_s, accu_s, hid_s, acco_s, gu_v, d_v, sems):
    n_src, rows, width = pieces_ref.shape
    tile = g_hbm.shape[1]
    gate_copy = pltpu.make_async_copy(g_hbm, gu_v.at[:, :, 0:tile], sems.at[0])
    up_copy = pltpu.make_async_copy(u_hbm, gu_v.at[:, :, tile:2 * tile], sems.at[1])
    down_copy = pltpu.make_async_copy(d_hbm, d_v, sems.at[2])
    gate_copy.start()
    up_copy.start()
    down_copy.start()
    per_src = width // tile
    feat = n_src * width
    ss = jnp.zeros((rows, 1), jnp.float32)
    for s in range(n_src):
        x = pieces_ref[s].astype(jnp.float32)
        ss = ss + jnp.sum(x * x, axis=1, keepdims=True)
    scale = lax.rsqrt(ss / feat + 1e-05)
    for s in range(n_src):
        for h in range(per_src):
            x = pieces_ref[s, :, h * tile:(h + 1) * tile].astype(jnp.float32)
            normed_s[s * per_src + h] = (x * scale).astype(jnp.bfloat16)
    accg_s[...] = jnp.zeros(accg_s.shape, jnp.float32)
    accu_s[...] = jnp.zeros(accu_s.shape, jnp.float32)
    gate_copy.wait()
    up_copy.wait()

    def gu_body(m, carry):
        x = normed_s[gu_ref[0, m]]
        h = gu_ref[1, m]
        live = (m < cnt_ref[0]).astype(jnp.float32)
        both = jnp.dot(x, gu_v[m], preferred_element_type=jnp.float32) * live
        accg_s[h] += both[:, :tile]
        accu_s[h] += both[:, tile:]
        return carry

    lax.fori_loop(0, gu_v.shape[0], gu_body, 0, unroll=UNROLL)
    g = accg_s[...]
    hid_s[...] = (g / (1.0 + jnp.exp(-g)) * accu_s[...]).astype(jnp.bfloat16)
    acco_s[...] = jnp.zeros(acco_s.shape, jnp.float32)
    down_copy.wait()

    def dn_body(m, carry):
        o = dn_ref[1, m]
        live = (m < cnt_ref[1]).astype(jnp.float32)
        acco_s[o] += jnp.dot(hid_s[dn_ref[0, m]], d_v[m], preferred_element_type=jnp.float32) * live
        return carry

    lax.fori_loop(0, d_v.shape[0], dn_body, 0, unroll=UNROLL)
    groups, dests, share, group_width = out_ref.shape
    rows = pl.ds(pl.multiple_of(me_ref[0] * share, share), share)
    per_group = group_width // tile
    for o in range(acco_s.shape[0]):
        acco_s[o, rows, :] += res_ref[:, o * tile:(o + 1) * tile]
        block = acco_s[o].reshape(dests, share, tile).astype(out_ref.dtype)
        group, half = divmod(o, per_group)
        out_ref[group, :, :, half * tile:(half + 1) * tile] = block


def ffn(counts, gu_blocks, down_blocks, me, pieces, gate_tiles, up_tiles, down_tiles, residual,
        hid_blocks, groups):
    n_src, rows, width = pieces.shape
    tile = gate_tiles.shape[1]
    in_blocks = n_src * width // tile
    share = residual.shape[0]
    smem = pl.BlockSpec(memory_space=pltpu.SMEM)
    vmem = pl.BlockSpec(memory_space=pltpu.VMEM)
    hbm = pl.BlockSpec(memory_space=pl.ANY)
    slots = gate_tiles.shape[0]
    return pl.pallas_call(
        ffn_kernel,
        out_shape=jax.ShapeDtypeStruct((groups, rows // share, share, in_blocks * tile // groups),
                                       jnp.bfloat16),
        in_specs=[smem, smem, smem, smem, vmem, hbm, hbm, hbm, vmem],
        out_specs=vmem,
        scratch_shapes=[
            pltpu.VMEM((in_blocks, rows, tile), jnp.bfloat16),
            pltpu.VMEM((hid_blocks, rows, tile), jnp.float32),
            pltpu.VMEM((hid_blocks, rows, tile), jnp.float32),
            pltpu.VMEM((hid_blocks, rows, tile), jnp.bfloat16),
            pltpu.VMEM((in_blocks, rows, tile), jnp.float32),
            pltpu.VMEM((slots, tile, 2 * tile), jnp.bfloat16),
            pltpu.VMEM((slots, tile, tile), jnp.bfloat16),
            pltpu.SemaphoreType.DMA((3,)),
        ],
    )(counts.reshape(-1), gu_blocks, down_blocks, me.reshape(1), pieces, gate_tiles, up_tiles,
      down_tiles, residual)

def ring_pairs(count, step):
    return [(i, ((i // Y_LO + step) % count) * Y_LO + i % Y_LO) for i in range(count * Y_LO)]


def per_device(tokens, gate_tiles, up_tiles, down_tiles, gu_blocks, down_blocks, counts):
    tp_count = lax.axis_size("tp")
    ctx_count = lax.axis_size("ctx")
    z_count = tp_count // Y_LO
    own_rows, own_width = tokens.shape
    tile = gate_tiles.shape[1]
    per_src = own_width // tile
    me = lax.axis_index("tp")
    my_z = me // Y_LO
    my_y = me % Y_LO
    partner = lax.ppermute(tokens, "tp", [(i, i ^ 1) for i in range(tp_count)])
    both = jnp.where(my_y == 0, jnp.stack([tokens, partner]), jnp.stack([partner, tokens]))
    ahead, behind = [], []
    fwd = bwd = both
    for k in range(1, z_count // 2 + 1):
        fwd = lax.ppermute(fwd, "tp", ring_pairs(z_count, 1))
        ahead.append(fwd)
        if k < z_count - z_count // 2:
            bwd = lax.ppermute(bwd, "tp", ring_pairs(z_count, -1))
            behind.append(bwd)
    pieces = jnp.concatenate([both] + ahead + behind)
    src_ids = jnp.arange(tp_count)
    dz = (src_ids // Y_LO - my_z) % z_count
    slot_of_z = jnp.where(dz == 0, 0, jnp.where(dz >= z_count // 2, z_count - dz, z_count // 2 + dz))
    position = slot_of_z * Y_LO + src_ids % Y_LO
    in_tile = gu_blocks[0]
    moved = position[in_tile // per_src] * per_src + in_tile % per_src
    gu_local = jnp.stack([moved, gu_blocks[1]])
    feat_width = tp_count * own_width
    in_blocks = feat_width // tile
    hid_blocks = FF // tp_count // tile
    share = own_rows // tp_count
    own = jnp.take(lax.dynamic_slice_in_dim(pieces, me * share, share, 1), position, axis=0)
    residual = jnp.transpose(own, (1, 0, 2)).reshape(share, feat_width).astype(jnp.float32)
    outgoing = ffn(counts, gu_local, down_blocks, me.astype(jnp.int32), pieces, gate_tiles,
                   up_tiles, down_tiles, residual, hid_blocks, ctx_count)
    incoming = lax.all_to_all(
        outgoing.reshape(ctx_count * tp_count, share, feat_width // ctx_count),
        ("ctx", "tp"), 0, 0, tiled=True,
    )
    total = jnp.sum(
        incoming.reshape(ctx_count, tp_count, share, -1).astype(jnp.float32), axis=1
    )
    return jnp.transpose(total, (1, 0, 2)).astype(jnp.bfloat16)

def solution(mesh):
    return jax.shard_map(
        per_device,
        mesh=mesh,
        in_specs=(
            P("ctx", "tp"),
            P("tp", None, None),
            P("tp", None, None),
            P("tp", None, None),
            P(None, "tp"),
            P(None, "tp"),
            P(None, "tp"),
        ),
        out_specs=P("tp", None, "ctx"),
        check_vma=False,
    )
```

```python
import jax
import jax.numpy as jnp
from jax import lax
from jax.experimental import pallas as pl
from jax.experimental.pallas import tpu as pltpu
from jax.sharding import PartitionSpec as P

FF = 16384
Y_LO = 2
CHUNKS = 8


def ffn_kernel(cnt_ref, gu_ref, dn_ref, me_ref, pieces_ref, g_hbm, u_hbm, d_hbm, res_ref, out_ref,
               normed_s, accg_s, accu_s, hid_s, acco_s, gu_v, d_v, sems):
    n_src, rows, width = pieces_ref.shape
    tile = g_hbm.shape[1]
    slots = g_hbm.shape[0]
    step = slots // CHUNKS
    copies = []
    for k in range(CHUNKS):
        part = pl.ds(k * step, step)
        copies.append((
            pltpu.make_async_copy(g_hbm.at[part], gu_v.at[part, :, 0:tile], sems.at[0, k]),
            pltpu.make_async_copy(u_hbm.at[part], gu_v.at[part, :, tile:2 * tile], sems.at[1, k]),
        ))
    down_copies = [
        pltpu.make_async_copy(d_hbm.at[pl.ds(k * step, step)], d_v.at[pl.ds(k * step, step)],
                              sems.at[2, k])
        for k in range(CHUNKS)
    ]
    for gate_copy, up_copy in copies:
        gate_copy.start()
        up_copy.start()
    for down_copy in down_copies:
        down_copy.start()
    per_src = width // tile
    feat = n_src * width
    ss = jnp.zeros((rows, 1), jnp.float32)
    for s in range(n_src):
        x = pieces_ref[s].astype(jnp.float32)
        ss = ss + jnp.sum(x * x, axis=1, keepdims=True)
    scale = lax.rsqrt(ss / feat + 1e-05)
    for s in range(n_src):
        for h in range(per_src):
            x = pieces_ref[s, :, h * tile:(h + 1) * tile].astype(jnp.float32)
            normed_s[s * per_src + h] = (x * scale).astype(jnp.bfloat16)
    accg_s[...] = jnp.zeros(accg_s.shape, jnp.float32)
    accu_s[...] = jnp.zeros(accu_s.shape, jnp.float32)

    def gu_body(m, carry):
        x = normed_s[gu_ref[0, m]]
        h = gu_ref[1, m]
        live = (m < cnt_ref[0]).astype(jnp.float32)
        both = jnp.dot(x, gu_v[m], preferred_element_type=jnp.float32) * live
        accg_s[h] += both[:, :tile]
        accu_s[h] += both[:, tile:]
        return carry

    for k, (gate_copy, up_copy) in enumerate(copies):
        gate_copy.wait()
        up_copy.wait()
        lax.fori_loop(k * step, (k + 1) * step, gu_body, 0, unroll=True)
    g = accg_s[...]
    hid_s[...] = (g / (1.0 + jnp.exp(-g)) * accu_s[...]).astype(jnp.bfloat16)
    acco_s[...] = jnp.zeros(acco_s.shape, jnp.float32)

    def dn_body(m, carry):
        o = dn_ref[1, m]
        live = (m < cnt_ref[1]).astype(jnp.float32)
        acco_s[o] += jnp.dot(hid_s[dn_ref[0, m]], d_v[m], preferred_element_type=jnp.float32) * live
        return carry

    for k, down_copy in enumerate(down_copies):
        down_copy.wait()
        lax.fori_loop(k * step, (k + 1) * step, dn_body, 0, unroll=True)
    groups, dests, share, group_width = out_ref.shape
    rows = pl.ds(pl.multiple_of(me_ref[0] * share, share), share)
    per_group = group_width // tile
    for o in range(acco_s.shape[0]):
        acco_s[o, rows, :] += res_ref[:, o * tile:(o + 1) * tile]
        block = acco_s[o].reshape(dests, share, tile).astype(out_ref.dtype)
        group, half = divmod(o, per_group)
        out_ref[group, :, :, half * tile:(half + 1) * tile] = block


def ffn(counts, gu_blocks, down_blocks, me, pieces, gate_tiles, up_tiles, down_tiles, residual,
        hid_blocks, groups):
    n_src, rows, width = pieces.shape
    tile = gate_tiles.shape[1]
    in_blocks = n_src * width // tile
    share = residual.shape[0]
    smem = pl.BlockSpec(memory_space=pltpu.SMEM)
    vmem = pl.BlockSpec(memory_space=pltpu.VMEM)
    hbm = pl.BlockSpec(memory_space=pl.ANY)
    slots = gate_tiles.shape[0]
    return pl.pallas_call(
        ffn_kernel,
        out_shape=jax.ShapeDtypeStruct((groups, rows // share, share, in_blocks * tile // groups),
                                       jnp.bfloat16),
        in_specs=[smem, smem, smem, smem, vmem, hbm, hbm, hbm, vmem],
        out_specs=vmem,
        scratch_shapes=[
            pltpu.VMEM((in_blocks, rows, tile), jnp.bfloat16),
            pltpu.VMEM((hid_blocks, rows, tile), jnp.float32),
            pltpu.VMEM((hid_blocks, rows, tile), jnp.float32),
            pltpu.VMEM((hid_blocks, rows, tile), jnp.bfloat16),
            pltpu.VMEM((in_blocks, rows, tile), jnp.float32),
            pltpu.VMEM((slots, tile, 2 * tile), jnp.bfloat16),
            pltpu.VMEM((slots, tile, tile), jnp.bfloat16),
            pltpu.SemaphoreType.DMA((3, CHUNKS)),
        ],
    )(counts.reshape(-1), gu_blocks, down_blocks, me.reshape(1), pieces, gate_tiles, up_tiles,
      down_tiles, residual)

def ring_pairs(count, step):
    return [(i, ((i // Y_LO + step) % count) * Y_LO + i % Y_LO) for i in range(count * Y_LO)]


def per_device(tokens, gate_tiles, up_tiles, down_tiles, gu_blocks, down_blocks, counts):
    tp_count = lax.axis_size("tp")
    ctx_count = lax.axis_size("ctx")
    z_count = tp_count // Y_LO
    own_rows, own_width = tokens.shape
    tile = gate_tiles.shape[1]
    per_src = own_width // tile
    me = lax.axis_index("tp")
    my_z = me // Y_LO
    my_y = me % Y_LO
    swap = [(i, i ^ 1) for i in range(tp_count)]
    half = z_count // 2
    arrays = [tokens[None], lax.ppermute(tokens, "tp", swap)[None]]
    origins = [(0, 0), (0, 1)]
    fwd = bwd = tokens
    for k in range(1, half + 1):
        fwd = lax.ppermute(fwd, "tp", ring_pairs(z_count, 1))
        arrays.append(fwd[None])
        origins.append((-k % z_count, 0))
        if k < z_count - half:
            bwd = lax.ppermute(bwd, "tp", ring_pairs(z_count, -1))
            arrays.append(bwd[None])
            origins.append((k, 0))
            arrays.append(lax.ppermute(jnp.stack([fwd, bwd]), "tp", swap))
            origins += [(-k % z_count, 1), (k, 1)]
        else:
            arrays.append(lax.ppermute(fwd, "tp", swap)[None])
            origins.append((-k % z_count, 1))
    pieces = jnp.concatenate(arrays)
    table = [[0] * Y_LO for _ in range(z_count)]
    for index, (dz, dy) in enumerate(origins):
        table[dz][dy] = index
    src_ids = jnp.arange(tp_count)
    dz = (src_ids // Y_LO - my_z) % z_count
    dy = (src_ids % Y_LO != my_y).astype(jnp.int32)
    position = jnp.array(table, jnp.int32)[dz, dy]
    in_tile = gu_blocks[0]
    moved = position[in_tile // per_src] * per_src + in_tile % per_src
    gu_local = jnp.stack([moved, gu_blocks[1]])
    feat_width = tp_count * own_width
    in_blocks = feat_width // tile
    hid_blocks = FF // tp_count // tile
    share = own_rows // tp_count
    own = jnp.take(lax.dynamic_slice_in_dim(pieces, me * share, share, 1), position, axis=0)
    residual = jnp.transpose(own, (1, 0, 2)).reshape(share, feat_width).astype(jnp.float32)
    outgoing = ffn(counts, gu_local, down_blocks, me.astype(jnp.int32), pieces, gate_tiles,
                   up_tiles, down_tiles, residual, hid_blocks, ctx_count)
    incoming = lax.all_to_all(
        outgoing.reshape(ctx_count * tp_count, share, feat_width // ctx_count),
        ("ctx", "tp"), 0, 0, tiled=True,
    )
    total = jnp.sum(
        incoming.reshape(ctx_count, tp_count, share, -1).astype(jnp.float32), axis=1
    )
    return jnp.transpose(total, (1, 0, 2)).astype(jnp.bfloat16)


def solution(mesh):
    return jax.shard_map(
        per_device,
        mesh=mesh,
        in_specs=(
            P("ctx", "tp"),
            P("tp", None, None),
            P("tp", None, None),
            P("tp", None, None),
            P(None, "tp"),
            P(None, "tp"),
            P(None, "tp"),
        ),
        out_specs=P("tp", None, "ctx"),
        check_vma=False,
    )
```

```python
import jax
import jax.numpy as jnp
from jax import lax
from jax.experimental import pallas as pl
from jax.experimental.pallas import tpu as pltpu
from jax.sharding import PartitionSpec as P

FF = 16384
Y_LO = 2
CHUNKS = 8


def ffn_kernel(cnt_ref, gu_ref, dn_ref, me_ref, table_ref, pieces_ref, g_hbm, u_hbm, d_hbm, out_ref,
               normed_s, accg_s, accu_s, hid_s, acco_s, gu_v, d_v, sems):
    n_src, rows, width = pieces_ref.shape
    tile = g_hbm.shape[1]
    slots = g_hbm.shape[0]
    step = slots // CHUNKS
    copies = []
    for k in range(CHUNKS):
        part = pl.ds(k * step, step)
        copies.append((
            pltpu.make_async_copy(g_hbm.at[part], gu_v.at[part, :, 0:tile], sems.at[0, k]),
            pltpu.make_async_copy(u_hbm.at[part], gu_v.at[part, :, tile:2 * tile], sems.at[1, k]),
        ))
    down_copies = [
        pltpu.make_async_copy(d_hbm.at[pl.ds(k * step, step)], d_v.at[pl.ds(k * step, step)],
                              sems.at[2, k])
        for k in range(CHUNKS)
    ]
    for gate_copy, up_copy in copies:
        gate_copy.start()
        up_copy.start()
    for down_copy in down_copies:
        down_copy.start()
    per_src = width // tile
    feat = n_src * width
    ss = jnp.zeros((rows, 1), jnp.float32)
    for s in range(n_src):
        x = pieces_ref[s].astype(jnp.float32)
        ss = ss + jnp.sum(x * x, axis=1, keepdims=True)
    scale = lax.rsqrt(ss / feat + 1e-05)
    for s in range(n_src):
        for h in range(per_src):
            x = pieces_ref[s, :, h * tile:(h + 1) * tile].astype(jnp.float32)
            normed_s[s * per_src + h] = (x * scale).astype(jnp.bfloat16)
    accg_s[...] = jnp.zeros(accg_s.shape, jnp.float32)
    accu_s[...] = jnp.zeros(accu_s.shape, jnp.float32)

    z_count = n_src // Y_LO
    my_z = me_ref[0] // Y_LO
    my_y = me_ref[0] % Y_LO

    def gu_body(m, carry):
        in_tile = gu_ref[0, m]
        source = in_tile // per_src
        dz = (source // Y_LO - my_z + z_count) % z_count
        dy = jnp.where(source % Y_LO == my_y, 0, 1)
        x = normed_s[table_ref[dz * Y_LO + dy] * per_src + in_tile % per_src]
        h = gu_ref[1, m]
        live = (m < cnt_ref[0]).astype(jnp.float32)
        both = jnp.dot(x, gu_v[m], preferred_element_type=jnp.float32) * live
        accg_s[h] += both[:, :tile]
        accu_s[h] += both[:, tile:]
        return carry

    for k, (gate_copy, up_copy) in enumerate(copies):
        gate_copy.wait()
        up_copy.wait()
        lax.fori_loop(k * step, (k + 1) * step, gu_body, 0, unroll=True)
    g = accg_s[...]
    hid_s[...] = (g / (1.0 + jnp.exp(-g)) * accu_s[...]).astype(jnp.bfloat16)
    acco_s[...] = jnp.zeros(acco_s.shape, jnp.float32)

    def dn_body(m, carry):
        o = dn_ref[1, m]
        live = (m < cnt_ref[1]).astype(jnp.float32)
        acco_s[o] += jnp.dot(hid_s[dn_ref[0, m]], d_v[m], preferred_element_type=jnp.float32) * live
        return carry

    for k, down_copy in enumerate(down_copies):
        down_copy.wait()
        lax.fori_loop(k * step, (k + 1) * step, dn_body, 0, unroll=True)
    groups, dests, share, group_width = out_ref.shape
    for h in range(per_src):
        acco_s[me_ref[0] * per_src + h] += pieces_ref[0, :, h * tile:(h + 1) * tile].astype(jnp.float32)
    per_group = group_width // tile
    for o in range(acco_s.shape[0]):
        block = acco_s[o].reshape(dests, share, tile).astype(out_ref.dtype)
        group, half = divmod(o, per_group)
        out_ref[group, :, :, half * tile:(half + 1) * tile] = block


def ffn(counts, gu_blocks, down_blocks, me, table, pieces, gate_tiles, up_tiles, down_tiles,
        hid_blocks, groups, share):
    n_src, rows, width = pieces.shape
    tile = gate_tiles.shape[1]
    in_blocks = n_src * width // tile
    smem = pl.BlockSpec(memory_space=pltpu.SMEM)
    vmem = pl.BlockSpec(memory_space=pltpu.VMEM)
    hbm = pl.BlockSpec(memory_space=pl.ANY)
    slots = gate_tiles.shape[0]
    return pl.pallas_call(
        ffn_kernel,
        out_shape=jax.ShapeDtypeStruct((groups, rows // share, share, in_blocks * tile // groups),
                                       jnp.bfloat16),
        in_specs=[smem, smem, smem, smem, smem, vmem, hbm, hbm, hbm],
        out_specs=vmem,
        scratch_shapes=[
            pltpu.VMEM((in_blocks, rows, tile), jnp.bfloat16),
            pltpu.VMEM((hid_blocks, rows, tile), jnp.float32),
            pltpu.VMEM((hid_blocks, rows, tile), jnp.float32),
            pltpu.VMEM((hid_blocks, rows, tile), jnp.bfloat16),
            pltpu.VMEM((in_blocks, rows, tile), jnp.float32),
            pltpu.VMEM((slots, tile, 2 * tile), jnp.bfloat16),
            pltpu.VMEM((slots, tile, tile), jnp.bfloat16),
            pltpu.SemaphoreType.DMA((3, CHUNKS)),
        ],
    )(counts.reshape(-1), gu_blocks, down_blocks, me.reshape(1), table, pieces, gate_tiles,
      up_tiles, down_tiles)

def ring_pairs(count, step):
    return [(i, ((i // Y_LO + step) % count) * Y_LO + i % Y_LO) for i in range(count * Y_LO)]


def per_device(tokens, gate_tiles, up_tiles, down_tiles, gu_blocks, down_blocks, counts):
    tp_count = lax.axis_size("tp")
    ctx_count = lax.axis_size("ctx")
    z_count = tp_count // Y_LO
    own_rows, own_width = tokens.shape
    tile = gate_tiles.shape[1]
    per_src = own_width // tile
    me = lax.axis_index("tp")
    my_z = me // Y_LO
    my_y = me % Y_LO
    swap = [(i, i ^ 1) for i in range(tp_count)]
    half = z_count // 2
    arrays = [tokens[None], lax.ppermute(tokens, "tp", swap)[None]]
    origins = [(0, 0), (0, 1)]
    fwd = bwd = tokens
    for k in range(1, half + 1):
        fwd = lax.ppermute(fwd, "tp", ring_pairs(z_count, 1))
        arrays.append(fwd[None])
        origins.append((-k % z_count, 0))
        if k < z_count - half:
            bwd = lax.ppermute(bwd, "tp", ring_pairs(z_count, -1))
            arrays.append(bwd[None])
            origins.append((k, 0))
            arrays.append(lax.ppermute(jnp.stack([fwd, bwd]), "tp", swap))
            origins += [(-k % z_count, 1), (k, 1)]
        else:
            arrays.append(lax.ppermute(fwd, "tp", swap)[None])
            origins.append((-k % z_count, 1))
    pieces = jnp.concatenate(arrays)
    table = [[0] * Y_LO for _ in range(z_count)]
    for index, (dz, dy) in enumerate(origins):
        table[dz][dy] = index
    feat_width = tp_count * own_width
    hid_blocks = FF // tp_count // tile
    share = own_rows // tp_count
    outgoing = ffn(counts, gu_blocks, down_blocks, me.astype(jnp.int32),
                   jnp.array(table, jnp.int32).reshape(-1), pieces, gate_tiles, up_tiles,
                   down_tiles, hid_blocks, ctx_count, share)
    incoming = lax.all_to_all(
        outgoing.reshape(ctx_count * tp_count, share, feat_width // ctx_count),
        ("ctx", "tp"), 0, 0, tiled=True,
    )
    total = jnp.sum(
        incoming.reshape(ctx_count, tp_count, share, -1).astype(jnp.float32), axis=1
    )
    return jnp.transpose(total, (1, 0, 2)).astype(jnp.bfloat16)


def solution(mesh):
    return jax.shard_map(
        per_device,
        mesh=mesh,
        in_specs=(
            P("ctx", "tp"),
            P("tp", None, None),
            P("tp", None, None),
            P("tp", None, None),
            P(None, "tp"),
            P(None, "tp"),
            P(None, "tp"),
        ),
        out_specs=P("tp", None, "ctx"),
        check_vma=False,
    )
```

```python
import jax
import jax.numpy as jnp
from jax import lax
from jax.experimental import pallas as pl
from jax.experimental.pallas import tpu as pltpu
from jax.sharding import PartitionSpec as P

FF = 16384
Y_LO = 2
CHUNKS = 8


def ffn_kernel(cnt_ref, gu_ref, dn_ref, me_ref, table_ref, pieces_ref, g_hbm, u_hbm, d_hbm, out_ref,
               normed_s, accg_s, accu_s, hid_s, acco_s, gu_v, d_v, sems):
    n_src, rows, width = pieces_ref.shape
    tile = g_hbm.shape[1]
    slots = g_hbm.shape[0]
    step = slots // CHUNKS
    copies = []
    for k in range(CHUNKS):
        part = pl.ds(k * step, step)
        copies.append((
            pltpu.make_async_copy(g_hbm.at[part], gu_v.at[part, :, 0:tile], sems.at[0, k]),
            pltpu.make_async_copy(u_hbm.at[part], gu_v.at[part, :, tile:2 * tile], sems.at[1, k]),
        ))
    down_copies = [
        pltpu.make_async_copy(d_hbm.at[pl.ds(k * step, step)], d_v.at[pl.ds(k * step, step)],
                              sems.at[2, k])
        for k in range(CHUNKS)
    ]
    for gate_copy, up_copy in copies:
        gate_copy.start()
        up_copy.start()
    for down_copy in down_copies:
        down_copy.start()
    per_src = width // tile
    feat = n_src * width
    ss = jnp.zeros((rows, 1), jnp.float32)
    for s in range(n_src):
        x = pieces_ref[s].astype(jnp.float32)
        ss = ss + jnp.sum(x * x, axis=1, keepdims=True)
    scale = lax.rsqrt(ss / feat + 1e-05)
    for s in range(n_src):
        for h in range(per_src):
            x = pieces_ref[s, :, h * tile:(h + 1) * tile].astype(jnp.float32)
            normed_s[s * per_src + h] = (x * scale).astype(jnp.bfloat16)
    accg_s[...] = jnp.zeros(accg_s.shape, jnp.float32)
    accu_s[...] = jnp.zeros(accu_s.shape, jnp.float32)

    z_count = n_src // Y_LO
    my_z = me_ref[0] // Y_LO
    my_y = me_ref[0] % Y_LO

    def gu_body(m, carry):
        in_tile = gu_ref[0, m]
        source = in_tile // per_src
        dz = (source // Y_LO - my_z + z_count) % z_count
        dy = jnp.where(source % Y_LO == my_y, 0, 1)
        x = normed_s[table_ref[dz * Y_LO + dy] * per_src + in_tile % per_src]
        h = gu_ref[1, m]
        live = (m < cnt_ref[0]).astype(jnp.float32)
        both = jnp.dot(x, gu_v[m], preferred_element_type=jnp.float32) * live
        accg_s[h] += both[:, :tile]
        accu_s[h] += both[:, tile:]
        return carry

    for k, (gate_copy, up_copy) in enumerate(copies):
        gate_copy.wait()
        up_copy.wait()
        lax.fori_loop(k * step, (k + 1) * step, gu_body, 0, unroll=True)
    g = accg_s[...]
    hid_s[...] = (g / (1.0 + jnp.exp(-g)) * accu_s[...]).astype(jnp.bfloat16)
    acco_s[...] = jnp.zeros(acco_s.shape, jnp.float32)

    def dn_body(m, carry):
        o = dn_ref[1, m]
        live = (m < cnt_ref[1]).astype(jnp.float32)
        acco_s[o] += jnp.dot(hid_s[dn_ref[0, m]], d_v[m], preferred_element_type=jnp.float32) * live
        return carry

    for k, down_copy in enumerate(down_copies):
        down_copy.wait()
        lax.fori_loop(k * step, (k + 1) * step, dn_body, 0, unroll=True)
    groups, dests, share, group_width = out_ref.shape
    for h in range(per_src):
        acco_s[me_ref[0] * per_src + h] += pieces_ref[0, :, h * tile:(h + 1) * tile].astype(jnp.float32)
    per_group = group_width // tile
    for o in range(acco_s.shape[0]):
        block = acco_s[o].reshape(dests, share, tile).astype(out_ref.dtype)
        group, half = divmod(o, per_group)
        out_ref[group, :, :, half * tile:(half + 1) * tile] = block


def ffn(counts, gu_blocks, down_blocks, me, table, pieces, gate_tiles, up_tiles, down_tiles,
        hid_blocks, groups, share):
    n_src, rows, width = pieces.shape
    tile = gate_tiles.shape[1]
    in_blocks = n_src * width // tile
    smem = pl.BlockSpec(memory_space=pltpu.SMEM)
    vmem = pl.BlockSpec(memory_space=pltpu.VMEM)
    hbm = pl.BlockSpec(memory_space=pl.ANY)
    slots = gate_tiles.shape[0]
    return pl.pallas_call(
        ffn_kernel,
        out_shape=jax.ShapeDtypeStruct((groups, rows // share, share, in_blocks * tile // groups),
                                       jnp.bfloat16),
        in_specs=[smem, smem, smem, smem, smem, vmem, hbm, hbm, hbm],
        out_specs=vmem,
        scratch_shapes=[
            pltpu.VMEM((in_blocks, rows, tile), jnp.bfloat16),
            pltpu.VMEM((hid_blocks, rows, tile), jnp.float32),
            pltpu.VMEM((hid_blocks, rows, tile), jnp.float32),
            pltpu.VMEM((hid_blocks, rows, tile), jnp.bfloat16),
            pltpu.VMEM((in_blocks, rows, tile), jnp.float32),
            pltpu.VMEM((slots, tile, 2 * tile), jnp.bfloat16),
            pltpu.VMEM((slots, tile, tile), jnp.bfloat16),
            pltpu.SemaphoreType.DMA((3, CHUNKS)),
        ],
    )(counts.reshape(-1), gu_blocks, down_blocks, me.reshape(1), table, pieces, gate_tiles,
      up_tiles, down_tiles)

def ring_pairs(count, step, flip=0):
    return [(i, ((i // Y_LO + step) % count) * Y_LO + (i % Y_LO ^ flip)) for i in range(count * Y_LO)]


def per_device(tokens, gate_tiles, up_tiles, down_tiles, gu_blocks, down_blocks, counts):
    tp_count = lax.axis_size("tp")
    ctx_count = lax.axis_size("ctx")
    z_count = tp_count // Y_LO
    own_rows, own_width = tokens.shape
    tile = gate_tiles.shape[1]
    per_src = own_width // tile
    me = lax.axis_index("tp")
    my_z = me // Y_LO
    my_y = me % Y_LO
    swap = [(i, i ^ 1) for i in range(tp_count)]
    half = z_count // 2
    arrays = [tokens[None], lax.ppermute(tokens, "tp", swap)[None]]
    origins = [(0, 0), (0, 1)]
    fwd = bwd = tokens
    for k in range(1, half + 1):
        arrays.append(lax.ppermute(fwd, "tp", ring_pairs(z_count, 1, 1))[None])
        origins.append((-k % z_count, 1))
        fwd = lax.ppermute(fwd, "tp", ring_pairs(z_count, 1))
        arrays.append(fwd[None])
        origins.append((-k % z_count, 0))
        if k < z_count - half:
            arrays.append(lax.ppermute(bwd, "tp", ring_pairs(z_count, -1, 1))[None])
            origins.append((k, 1))
            bwd = lax.ppermute(bwd, "tp", ring_pairs(z_count, -1))
            arrays.append(bwd[None])
            origins.append((k, 0))
    pieces = jnp.concatenate(arrays)
    table = [[0] * Y_LO for _ in range(z_count)]
    for index, (dz, dy) in enumerate(origins):
        table[dz][dy] = index
    feat_width = tp_count * own_width
    hid_blocks = FF // tp_count // tile
    share = own_rows // tp_count
    outgoing = ffn(counts, gu_blocks, down_blocks, me.astype(jnp.int32),
                   jnp.array(table, jnp.int32).reshape(-1), pieces, gate_tiles, up_tiles,
                   down_tiles, hid_blocks, ctx_count, share)
    incoming = lax.all_to_all(
        outgoing.reshape(ctx_count * tp_count, share, feat_width // ctx_count),
        ("ctx", "tp"), 0, 0, tiled=True,
    )
    total = jnp.sum(
        incoming.reshape(ctx_count, tp_count, share, -1).astype(jnp.float32), axis=1
    )
    return jnp.transpose(total, (1, 0, 2)).astype(jnp.bfloat16)


def solution(mesh):
    return jax.shard_map(
        per_device,
        mesh=mesh,
        in_specs=(
            P("ctx", "tp"),
            P("tp", None, None),
            P("tp", None, None),
            P("tp", None, None),
            P(None, "tp"),
            P(None, "tp"),
            P(None, "tp"),
        ),
        out_specs=P("tp", None, "ctx"),
        check_vma=False,
    )
```

```python
import jax
import jax.numpy as jnp
from jax import lax
from jax.experimental import pallas as pl
from jax.experimental.pallas import tpu as pltpu
from jax.sharding import PartitionSpec as P

FF = 16384
Y_LO = 2
CHUNKS = 8


def ffn_kernel(cnt_ref, gu_ref, dn_ref, me_ref, table_ref, *refs):
    n_src = table_ref.shape[0]
    piece_refs = refs[:n_src]
    (g_hbm, u_hbm, d_hbm, out_ref, normed_s, accg_s, accu_s, hid_s, acco_s, gu_v, d_v,
     sems) = refs[n_src:]
    rows, width = piece_refs[0].shape
    tile = g_hbm.shape[1]
    slots = g_hbm.shape[0]
    step = slots // CHUNKS
    copies = []
    for k in range(CHUNKS):
        part = pl.ds(k * step, step)
        copies.append((
            pltpu.make_async_copy(g_hbm.at[part], gu_v.at[part, :, 0:tile], sems.at[0, k]),
            pltpu.make_async_copy(u_hbm.at[part], gu_v.at[part, :, tile:2 * tile], sems.at[1, k]),
        ))
    down_copies = [
        pltpu.make_async_copy(d_hbm.at[pl.ds(k * step, step)], d_v.at[pl.ds(k * step, step)],
                              sems.at[2, k])
        for k in range(CHUNKS)
    ]
    for gate_copy, up_copy in copies:
        gate_copy.start()
        up_copy.start()
    for down_copy in down_copies:
        down_copy.start()
    per_src = width // tile
    feat = n_src * width
    ss = jnp.zeros((rows, 1), jnp.float32)
    for s in range(n_src):
        x = piece_refs[s][...].astype(jnp.float32)
        ss = ss + jnp.sum(x * x, axis=1, keepdims=True)
    scale = lax.rsqrt(ss / feat + 1e-05)
    for s in range(n_src):
        for h in range(per_src):
            x = piece_refs[s][:, h * tile:(h + 1) * tile].astype(jnp.float32)
            normed_s[s * per_src + h] = (x * scale).astype(jnp.bfloat16)
    accg_s[...] = jnp.zeros(accg_s.shape, jnp.float32)
    accu_s[...] = jnp.zeros(accu_s.shape, jnp.float32)

    z_count = n_src // Y_LO
    my_z = me_ref[0] // Y_LO
    my_y = me_ref[0] % Y_LO

    def gu_body(m, carry):
        in_tile = gu_ref[0, m]
        source = in_tile // per_src
        dz = (source // Y_LO - my_z + z_count) % z_count
        dy = jnp.where(source % Y_LO == my_y, 0, 1)
        x = normed_s[table_ref[dz * Y_LO + dy] * per_src + in_tile % per_src]
        h = gu_ref[1, m]
        live = (m < cnt_ref[0]).astype(jnp.float32)
        both = jnp.dot(x, gu_v[m], preferred_element_type=jnp.float32) * live
        accg_s[h] += both[:, :tile]
        accu_s[h] += both[:, tile:]
        return carry

    for k, (gate_copy, up_copy) in enumerate(copies):
        gate_copy.wait()
        up_copy.wait()
        lax.fori_loop(k * step, (k + 1) * step, gu_body, 0, unroll=True)
    g = accg_s[...]
    hid_s[...] = (g / (1.0 + jnp.exp(-g)) * accu_s[...]).astype(jnp.bfloat16)
    acco_s[...] = jnp.zeros(acco_s.shape, jnp.float32)

    def dn_body(m, carry):
        o = dn_ref[1, m]
        live = (m < cnt_ref[1]).astype(jnp.float32)
        acco_s[o] += jnp.dot(hid_s[dn_ref[0, m]], d_v[m], preferred_element_type=jnp.float32) * live
        return carry

    for k, down_copy in enumerate(down_copies):
        down_copy.wait()
        lax.fori_loop(k * step, (k + 1) * step, dn_body, 0, unroll=True)
    groups, dests, share, group_width = out_ref.shape
    for h in range(per_src):
        acco_s[me_ref[0] * per_src + h] += piece_refs[0][:, h * tile:(h + 1) * tile].astype(jnp.float32)
    per_group = group_width // tile
    for o in range(acco_s.shape[0]):
        block = acco_s[o].reshape(dests, share, tile).astype(out_ref.dtype)
        group, half = divmod(o, per_group)
        out_ref[group, :, :, half * tile:(half + 1) * tile] = block


def ffn(counts, gu_blocks, down_blocks, me, table, pieces, gate_tiles, up_tiles, down_tiles,
        hid_blocks, groups, share):
    n_src = len(pieces)
    rows, width = pieces[0].shape
    tile = gate_tiles.shape[1]
    in_blocks = n_src * width // tile
    smem = pl.BlockSpec(memory_space=pltpu.SMEM)
    vmem = pl.BlockSpec(memory_space=pltpu.VMEM)
    hbm = pl.BlockSpec(memory_space=pl.ANY)
    slots = gate_tiles.shape[0]
    return pl.pallas_call(
        ffn_kernel,
        out_shape=jax.ShapeDtypeStruct((groups, rows // share, share, in_blocks * tile // groups),
                                       jnp.bfloat16),
        in_specs=[smem] * 5 + [vmem] * n_src + [hbm] * 3,
        out_specs=vmem,
        scratch_shapes=[
            pltpu.VMEM((in_blocks, rows, tile), jnp.bfloat16),
            pltpu.VMEM((hid_blocks, rows, tile), jnp.float32),
            pltpu.VMEM((hid_blocks, rows, tile), jnp.float32),
            pltpu.VMEM((hid_blocks, rows, tile), jnp.bfloat16),
            pltpu.VMEM((in_blocks, rows, tile), jnp.float32),
            pltpu.VMEM((slots, tile, 2 * tile), jnp.bfloat16),
            pltpu.VMEM((slots, tile, tile), jnp.bfloat16),
            pltpu.SemaphoreType.DMA((3, CHUNKS)),
        ],
    )(counts.reshape(-1), gu_blocks, down_blocks, me.reshape(1), table, *pieces, gate_tiles,
      up_tiles, down_tiles)

def ring_pairs(count, step, flip=0):
    return [(i, ((i // Y_LO + step) % count) * Y_LO + (i % Y_LO ^ flip)) for i in range(count * Y_LO)]


def per_device(tokens, gate_tiles, up_tiles, down_tiles, gu_blocks, down_blocks, counts):
    tp_count = lax.axis_size("tp")
    ctx_count = lax.axis_size("ctx")
    z_count = tp_count // Y_LO
    own_rows, own_width = tokens.shape
    tile = gate_tiles.shape[1]
    per_src = own_width // tile
    me = lax.axis_index("tp")
    my_z = me // Y_LO
    my_y = me % Y_LO
    swap = [(i, i ^ 1) for i in range(tp_count)]
    half = z_count // 2
    arrays = [tokens, lax.ppermute(tokens, "tp", swap)]
    origins = [(0, 0), (0, 1)]
    fwd = bwd = tokens
    for k in range(1, half + 1):
        arrays.append(lax.ppermute(fwd, "tp", ring_pairs(z_count, 1, 1)))
        origins.append((-k % z_count, 1))
        fwd = lax.ppermute(fwd, "tp", ring_pairs(z_count, 1))
        arrays.append(fwd)
        origins.append((-k % z_count, 0))
        if k < z_count - half:
            arrays.append(lax.ppermute(bwd, "tp", ring_pairs(z_count, -1, 1)))
            origins.append((k, 1))
            bwd = lax.ppermute(bwd, "tp", ring_pairs(z_count, -1))
            arrays.append(bwd)
            origins.append((k, 0))
    table = [[0] * Y_LO for _ in range(z_count)]
    for index, (dz, dy) in enumerate(origins):
        table[dz][dy] = index
    feat_width = tp_count * own_width
    hid_blocks = FF // tp_count // tile
    share = own_rows // tp_count
    outgoing = ffn(counts, gu_blocks, down_blocks, me.astype(jnp.int32),
                   jnp.array(table, jnp.int32).reshape(-1), arrays, gate_tiles, up_tiles,
                   down_tiles, hid_blocks, ctx_count, share)
    incoming = lax.all_to_all(
        outgoing.reshape(ctx_count * tp_count, share, feat_width // ctx_count),
        ("ctx", "tp"), 0, 0, tiled=True,
    )
    total = jnp.sum(
        incoming.reshape(ctx_count, tp_count, share, -1).astype(jnp.float32), axis=1
    )
    return jnp.transpose(total, (1, 0, 2)).astype(jnp.bfloat16)


def solution(mesh):
    return jax.shard_map(
        per_device,
        mesh=mesh,
        in_specs=(
            P("ctx", "tp"),
            P("tp", None, None),
            P("tp", None, None),
            P("tp", None, None),
            P(None, "tp"),
            P(None, "tp"),
            P(None, "tp"),
        ),
        out_specs=P("tp", None, "ctx"),
        check_vma=False,
    )
```

```python
import jax
import jax.numpy as jnp
from jax import lax
from jax.experimental import pallas as pl
from jax.experimental.pallas import tpu as pltpu
from jax.sharding import PartitionSpec as P

FF = 16384
Y_LO = 2
CHUNKS = 8


def ffn_kernel(cnt_ref, gu_ref, dn_ref, me_ref, table_ref, *refs):
    n_src = table_ref.shape[0]
    piece_refs = refs[:n_src]
    (g_hbm, u_hbm, d_hbm, out_ref, normed_s, accg_s, accu_s, hid_s, acco_s, gu_v, d_v,
     sems) = refs[n_src:]
    rows, width = piece_refs[0].shape
    tile = g_hbm.shape[1]
    slots = g_hbm.shape[0]
    step = slots // CHUNKS
    copies = []
    for k in range(CHUNKS):
        part = pl.ds(k * step, step)
        copies.append((
            pltpu.make_async_copy(g_hbm.at[part], gu_v.at[part, :, 0:tile], sems.at[0, k]),
            pltpu.make_async_copy(u_hbm.at[part], gu_v.at[part, :, tile:2 * tile], sems.at[1, k]),
        ))
    down_copies = [
        pltpu.make_async_copy(d_hbm.at[pl.ds(k * step, step)], d_v.at[pl.ds(k * step, step)],
                              sems.at[2, k])
        for k in range(CHUNKS)
    ]
    for gate_copy, up_copy in copies:
        gate_copy.start()
        up_copy.start()
    for down_copy in down_copies:
        down_copy.start()
    per_src = width // tile
    feat = n_src * width
    ss = jnp.zeros((rows, 1), jnp.float32)
    for s in range(n_src):
        x = piece_refs[s][...].astype(jnp.float32)
        ss = ss + jnp.sum(x * x, axis=1, keepdims=True)
    scale = lax.rsqrt(ss / feat + 1e-05)
    for s in range(n_src):
        for h in range(per_src):
            x = piece_refs[s][:, h * tile:(h + 1) * tile].astype(jnp.float32)
            normed_s[s * per_src + h] = (x * scale).astype(jnp.bfloat16)
    accg_s[...] = jnp.zeros(accg_s.shape, jnp.float32)
    accu_s[...] = jnp.zeros(accu_s.shape, jnp.float32)

    z_count = n_src // Y_LO
    my_z = me_ref[0] // Y_LO
    my_y = me_ref[0] % Y_LO

    def gu_body(m, carry):
        in_tile = gu_ref[0, m]
        source = in_tile // per_src
        dz = (source // Y_LO - my_z + z_count) % z_count
        dy = jnp.where(source % Y_LO == my_y, 0, 1)
        x = normed_s[table_ref[dz * Y_LO + dy] * per_src + in_tile % per_src]
        h = gu_ref[1, m]
        live = (m < cnt_ref[0]).astype(jnp.float32)
        both = jnp.dot(x, gu_v[m], preferred_element_type=jnp.float32) * live
        accg_s[h] += both[:, :tile]
        accu_s[h] += both[:, tile:]
        return carry

    for k, (gate_copy, up_copy) in enumerate(copies):
        gate_copy.wait()
        up_copy.wait()
        lax.fori_loop(k * step, (k + 1) * step, gu_body, 0, unroll=True)
    g = accg_s[...]
    hid_s[...] = (g / (1.0 + jnp.exp(-g)) * accu_s[...]).astype(jnp.bfloat16)
    acco_s[...] = jnp.zeros(acco_s.shape, jnp.float32)

    def dn_body(m, carry):
        o = dn_ref[1, m]
        live = (m < cnt_ref[1]).astype(jnp.float32)
        acco_s[o] += jnp.dot(hid_s[dn_ref[0, m]], d_v[m], preferred_element_type=jnp.float32) * live
        return carry

    for k, down_copy in enumerate(down_copies):
        down_copy.wait()
        lax.fori_loop(k * step, (k + 1) * step, dn_body, 0, unroll=True)
    groups, dests, share, group_width = out_ref.shape
    for h in range(per_src):
        acco_s[me_ref[0] * per_src + h] += piece_refs[0][:, h * tile:(h + 1) * tile].astype(jnp.float32)
    per_group = group_width // tile
    for o in range(acco_s.shape[0]):
        block = acco_s[o].reshape(dests, share, tile).astype(out_ref.dtype)
        group, half = divmod(o, per_group)
        out_ref[group, :, :, half * tile:(half + 1) * tile] = block


def ffn(counts, gu_blocks, down_blocks, me, table, pieces, gate_tiles, up_tiles, down_tiles,
        hid_blocks, groups, share):
    n_src = len(pieces)
    rows, width = pieces[0].shape
    tile = gate_tiles.shape[1]
    in_blocks = n_src * width // tile
    smem = pl.BlockSpec(memory_space=pltpu.SMEM)
    vmem = pl.BlockSpec(memory_space=pltpu.VMEM)
    hbm = pl.BlockSpec(memory_space=pl.ANY)
    slots = gate_tiles.shape[0]
    return pl.pallas_call(
        ffn_kernel,
        out_shape=jax.ShapeDtypeStruct((groups, rows // share, share, in_blocks * tile // groups),
                                       jnp.bfloat16),
        in_specs=[smem] * 5 + [vmem] * n_src + [hbm] * 3,
        out_specs=vmem,
        scratch_shapes=[
            pltpu.VMEM((in_blocks, rows, tile), jnp.bfloat16),
            pltpu.VMEM((hid_blocks, rows, tile), jnp.float32),
            pltpu.VMEM((hid_blocks, rows, tile), jnp.float32),
            pltpu.VMEM((hid_blocks, rows, tile), jnp.bfloat16),
            pltpu.VMEM((in_blocks, rows, tile), jnp.float32),
            pltpu.VMEM((slots, tile, 2 * tile), jnp.bfloat16),
            pltpu.VMEM((slots, tile, tile), jnp.bfloat16),
            pltpu.SemaphoreType.DMA((3, CHUNKS)),
        ],
    )(counts.reshape(-1), gu_blocks, down_blocks, me.reshape(1), table, *pieces, gate_tiles,
      up_tiles, down_tiles)

def ring_pairs(count, step, flip=0):
    return [(i, ((i // Y_LO + step) % count) * Y_LO + (i % Y_LO ^ flip)) for i in range(count * Y_LO)]


def per_device(tokens, gate_tiles, up_tiles, down_tiles, gu_blocks, down_blocks, counts):
    tp_count = lax.axis_size("tp")
    ctx_count = lax.axis_size("ctx")
    z_count = tp_count // Y_LO
    own_rows, own_width = tokens.shape
    tile = gate_tiles.shape[1]
    per_src = own_width // tile
    me = lax.axis_index("tp")
    my_z = me // Y_LO
    my_y = me % Y_LO
    swap = [(i, i ^ 1) for i in range(tp_count)]
    arrays = [tokens, lax.ppermute(tokens, "tp", swap)]
    origins = [(0, 0), (0, 1)]
    near = {}
    for step in (1, -1):
        same = lax.ppermute(tokens, "tp", ring_pairs(z_count, step))
        other = lax.ppermute(tokens, "tp", ring_pairs(z_count, step, 1))
        arrays += [same, other]
        origins += [(-step % z_count, 0), (-step % z_count, 1)]
        near[step] = jnp.stack([same, other])
    far = {}
    for step in (1, -1):
        for hops in (1, 2):
            pair = lax.ppermute(near[step], "tp", ring_pairs(z_count, step * hops))
            arrays += [pair[0], pair[1]]
            origins += [(-step * (hops + 1) % z_count, 0), (-step * (hops + 1) % z_count, 1)]
            far[step, hops] = pair
    last = lax.ppermute(far[1, 2], "tp", ring_pairs(z_count, 1))
    arrays += [last[0], last[1]]
    origins += [(-4 % z_count, 0), (-4 % z_count, 1)]
    table = [[0] * Y_LO for _ in range(z_count)]
    for index, (dz, dy) in enumerate(origins):
        table[dz][dy] = index
    feat_width = tp_count * own_width
    hid_blocks = FF // tp_count // tile
    share = own_rows // tp_count
    outgoing = ffn(counts, gu_blocks, down_blocks, me.astype(jnp.int32),
                   jnp.array(table, jnp.int32).reshape(-1), arrays, gate_tiles, up_tiles,
                   down_tiles, hid_blocks, ctx_count, share)
    incoming = lax.all_to_all(
        outgoing.reshape(ctx_count * tp_count, share, feat_width // ctx_count),
        ("ctx", "tp"), 0, 0, tiled=True,
    )
    total = jnp.sum(
        incoming.reshape(ctx_count, tp_count, share, -1).astype(jnp.float32), axis=1
    )
    return jnp.transpose(total, (1, 0, 2)).astype(jnp.bfloat16)


def solution(mesh):
    return jax.shard_map(
        per_device,
        mesh=mesh,
        in_specs=(
            P("ctx", "tp"),
            P("tp", None, None),
            P("tp", None, None),
            P("tp", None, None),
            P(None, "tp"),
            P(None, "tp"),
            P(None, "tp"),
        ),
        out_specs=P("tp", None, "ctx"),
        check_vma=False,
    )
```

```python
import functools

import jax
import jax.numpy as jnp
from jax import lax
from jax.experimental import pallas as pl
from jax.experimental.pallas import tpu as pltpu
from jax.sharding import PartitionSpec as P

FF = 16384
Y_LO = 2
CHUNKS = 8


def ffn_kernel(layout, cnt_ref, gu_ref, dn_ref, me_ref, table_ref, *refs):
    n_src = len(layout)
    n_ops = len(refs) - 12
    piece_refs = refs[:n_ops]
    (g_hbm, u_hbm, d_hbm, out_ref, normed_s, accg_s, accu_s, hid_s, acco_s, gu_v, d_v,
     sems) = refs[n_ops:]
    rows, width = piece_refs[0].shape

    def piece(s, cols):
        ref = piece_refs[layout[s][0]]
        return ref[:, cols] if layout[s][1] < 0 else ref[layout[s][1], :, cols]

    tile = g_hbm.shape[1]
    slots = g_hbm.shape[0]
    step = slots // CHUNKS
    copies = []
    for k in range(CHUNKS):
        part = pl.ds(k * step, step)
        copies.append((
            pltpu.make_async_copy(g_hbm.at[part], gu_v.at[part, :, 0:tile], sems.at[0, k]),
            pltpu.make_async_copy(u_hbm.at[part], gu_v.at[part, :, tile:2 * tile], sems.at[1, k]),
        ))
    down_copies = [
        pltpu.make_async_copy(d_hbm.at[pl.ds(k * step, step)], d_v.at[pl.ds(k * step, step)],
                              sems.at[2, k])
        for k in range(CHUNKS)
    ]
    for gate_copy, up_copy in copies:
        gate_copy.start()
        up_copy.start()
    for down_copy in down_copies:
        down_copy.start()
    per_src = width // tile
    feat = n_src * width
    ss = jnp.zeros((rows, 1), jnp.float32)
    for s in range(n_src):
        x = piece(s, slice(None)).astype(jnp.float32)
        ss = ss + jnp.sum(x * x, axis=1, keepdims=True)
    scale = lax.rsqrt(ss / feat + 1e-05)
    for s in range(n_src):
        for h in range(per_src):
            x = piece(s, slice(h * tile, (h + 1) * tile)).astype(jnp.float32)
            normed_s[s * per_src + h] = (x * scale).astype(jnp.bfloat16)
    accg_s[...] = jnp.zeros(accg_s.shape, jnp.float32)
    accu_s[...] = jnp.zeros(accu_s.shape, jnp.float32)

    z_count = n_src // Y_LO
    my_z = me_ref[0] // Y_LO
    my_y = me_ref[0] % Y_LO

    def gu_body(m, carry):
        in_tile = gu_ref[0, m]
        source = in_tile // per_src
        dz = (source // Y_LO - my_z + z_count) % z_count
        dy = jnp.where(source % Y_LO == my_y, 0, 1)
        x = normed_s[table_ref[dz * Y_LO + dy] * per_src + in_tile % per_src]
        h = gu_ref[1, m]
        live = (m < cnt_ref[0]).astype(jnp.float32)
        both = jnp.dot(x, gu_v[m], preferred_element_type=jnp.float32) * live
        accg_s[h] += both[:, :tile]
        accu_s[h] += both[:, tile:]
        return carry

    for k, (gate_copy, up_copy) in enumerate(copies):
        gate_copy.wait()
        up_copy.wait()
        lax.fori_loop(k * step, (k + 1) * step, gu_body, 0, unroll=True)
    g = accg_s[...]
    hid_s[...] = (g / (1.0 + jnp.exp(-g)) * accu_s[...]).astype(jnp.bfloat16)
    acco_s[...] = jnp.zeros(acco_s.shape, jnp.float32)

    def dn_body(m, carry):
        o = dn_ref[1, m]
        live = (m < cnt_ref[1]).astype(jnp.float32)
        acco_s[o] += jnp.dot(hid_s[dn_ref[0, m]], d_v[m], preferred_element_type=jnp.float32) * live
        return carry

    for k, down_copy in enumerate(down_copies):
        down_copy.wait()
        lax.fori_loop(k * step, (k + 1) * step, dn_body, 0, unroll=True)
    groups, dests, share, group_width = out_ref.shape
    for h in range(per_src):
        acco_s[me_ref[0] * per_src + h] += piece(0, slice(h * tile, (h + 1) * tile)).astype(jnp.float32)
    per_group = group_width // tile
    for o in range(acco_s.shape[0]):
        block = acco_s[o].reshape(dests, share, tile).astype(out_ref.dtype)
        group, half = divmod(o, per_group)
        out_ref[group, :, :, half * tile:(half + 1) * tile] = block


def ffn(counts, gu_blocks, down_blocks, me, table, pieces, gate_tiles, up_tiles, down_tiles,
        hid_blocks, groups, share):
    layout = []
    for index, array in enumerate(pieces):
        layout += [(index, -1)] if array.ndim == 2 else [(index, sub) for sub in range(array.shape[0])]
    n_src = len(layout)
    rows, width = pieces[0].shape
    tile = gate_tiles.shape[1]
    in_blocks = n_src * width // tile
    smem = pl.BlockSpec(memory_space=pltpu.SMEM)
    vmem = pl.BlockSpec(memory_space=pltpu.VMEM)
    hbm = pl.BlockSpec(memory_space=pl.ANY)
    slots = gate_tiles.shape[0]
    return pl.pallas_call(
        functools.partial(ffn_kernel, tuple(layout)),
        out_shape=jax.ShapeDtypeStruct((groups, rows // share, share, in_blocks * tile // groups),
                                       jnp.bfloat16),
        in_specs=[smem] * 5 + [vmem] * len(pieces) + [hbm] * 3,
        out_specs=vmem,
        scratch_shapes=[
            pltpu.VMEM((in_blocks, rows, tile), jnp.bfloat16),
            pltpu.VMEM((hid_blocks, rows, tile), jnp.float32),
            pltpu.VMEM((hid_blocks, rows, tile), jnp.float32),
            pltpu.VMEM((hid_blocks, rows, tile), jnp.bfloat16),
            pltpu.VMEM((in_blocks, rows, tile), jnp.float32),
            pltpu.VMEM((slots, tile, 2 * tile), jnp.bfloat16),
            pltpu.VMEM((slots, tile, tile), jnp.bfloat16),
            pltpu.SemaphoreType.DMA((3, CHUNKS)),
        ],
    )(counts.reshape(-1), gu_blocks, down_blocks, me.reshape(1), table, *pieces, gate_tiles,
      up_tiles, down_tiles)

def ring_pairs(count, step, flip=0):
    return [(i, ((i // Y_LO + step) % count) * Y_LO + (i % Y_LO ^ flip)) for i in range(count * Y_LO)]


def per_device(tokens, gate_tiles, up_tiles, down_tiles, gu_blocks, down_blocks, counts):
    tp_count = lax.axis_size("tp")
    ctx_count = lax.axis_size("ctx")
    z_count = tp_count // Y_LO
    own_rows, own_width = tokens.shape
    tile = gate_tiles.shape[1]
    per_src = own_width // tile
    me = lax.axis_index("tp")
    my_z = me // Y_LO
    my_y = me % Y_LO
    swap = [(i, i ^ 1) for i in range(tp_count)]
    arrays = [tokens, lax.ppermute(tokens, "tp", swap)]
    origins = [(0, 0), (0, 1)]
    near = {}
    for step in (1, -1):
        same = lax.ppermute(tokens, "tp", ring_pairs(z_count, step))
        other = lax.ppermute(tokens, "tp", ring_pairs(z_count, step, 1))
        arrays += [same, other]
        origins += [(-step % z_count, 0), (-step % z_count, 1)]
        near[step] = jnp.stack([same, other])
    far = {}
    for step in (1, -1):
        for hops in (1, 2):
            pair = lax.ppermute(near[step], "tp", ring_pairs(z_count, step * hops))
            arrays.append(pair)
            origins += [(-step * (hops + 1) % z_count, 0), (-step * (hops + 1) % z_count, 1)]
            far[step, hops] = pair
    last = lax.ppermute(far[1, 2], "tp", ring_pairs(z_count, 1))
    arrays.append(last)
    origins += [(-4 % z_count, 0), (-4 % z_count, 1)]
    table = [[0] * Y_LO for _ in range(z_count)]
    for index, (dz, dy) in enumerate(origins):
        table[dz][dy] = index
    feat_width = tp_count * own_width
    hid_blocks = FF // tp_count // tile
    share = own_rows // tp_count
    outgoing = ffn(counts, gu_blocks, down_blocks, me.astype(jnp.int32),
                   jnp.array(table, jnp.int32).reshape(-1), arrays, gate_tiles, up_tiles,
                   down_tiles, hid_blocks, ctx_count, share)
    incoming = lax.all_to_all(
        outgoing.reshape(ctx_count * tp_count, share, feat_width // ctx_count),
        ("ctx", "tp"), 0, 0, tiled=True,
    )
    total = jnp.sum(
        incoming.reshape(ctx_count, tp_count, share, -1).astype(jnp.float32), axis=1
    )
    return jnp.transpose(total, (1, 0, 2)).astype(jnp.bfloat16)


def solution(mesh):
    return jax.shard_map(
        per_device,
        mesh=mesh,
        in_specs=(
            P("ctx", "tp"),
            P("tp", None, None),
            P("tp", None, None),
            P("tp", None, None),
            P(None, "tp"),
            P(None, "tp"),
            P(None, "tp"),
        ),
        out_specs=P("tp", None, "ctx"),
        check_vma=False,
    )
```

```python
import functools

import jax
import jax.numpy as jnp
from jax import lax
from jax.experimental import pallas as pl
from jax.experimental.pallas import tpu as pltpu
from jax.sharding import PartitionSpec as P

FF = 16384
Y_LO = 2
CHUNKS = 8


def ffn_kernel(layout, cnt_ref, gu_ref, dn_ref, me_ref, table_ref, *refs):
    n_src = len(layout)
    n_ops = len(refs) - 12
    piece_refs = refs[:n_ops]
    (g_hbm, u_hbm, d_hbm, out_ref, normed_s, accg_s, accu_s, hid_s, acco_s, gu_v, d_v,
     sems) = refs[n_ops:]
    rows, width = piece_refs[0].shape

    def piece(s, cols):
        ref = piece_refs[layout[s][0]]
        return ref[:, cols] if layout[s][1] < 0 else ref[layout[s][1], :, cols]

    tile = g_hbm.shape[1]
    slots = g_hbm.shape[0]
    step = slots // CHUNKS
    copies = []
    for k in range(CHUNKS):
        part = pl.ds(k * step, step)
        copies.append((
            pltpu.make_async_copy(g_hbm.at[part], gu_v.at[part, :, 0:tile], sems.at[0, k]),
            pltpu.make_async_copy(u_hbm.at[part], gu_v.at[part, :, tile:2 * tile], sems.at[1, k]),
        ))
    down_copies = [
        pltpu.make_async_copy(d_hbm.at[pl.ds(k * step, step)], d_v.at[pl.ds(k * step, step)],
                              sems.at[2, k])
        for k in range(CHUNKS)
    ]
    for gate_copy, up_copy in copies:
        gate_copy.start()
        up_copy.start()
    for down_copy in down_copies:
        down_copy.start()
    per_src = width // tile
    feat = n_src * width
    ss = jnp.zeros((rows, 1), jnp.float32)
    for s in range(n_src):
        x = piece(s, slice(None)).astype(jnp.float32)
        ss = ss + jnp.sum(x * x, axis=1, keepdims=True)
    scale = lax.rsqrt(ss / feat + 1e-05)
    for s in range(n_src):
        for h in range(per_src):
            x = piece(s, slice(h * tile, (h + 1) * tile)).astype(jnp.float32)
            normed_s[s * per_src + h] = (x * scale).astype(jnp.bfloat16)
    accg_s[...] = jnp.zeros(accg_s.shape, jnp.float32)
    accu_s[...] = jnp.zeros(accu_s.shape, jnp.float32)

    z_count = n_src // Y_LO
    my_z = me_ref[0] // Y_LO
    my_y = me_ref[0] % Y_LO

    def gu_body(m, carry):
        in_tile = gu_ref[0, m]
        source = in_tile // per_src
        dz = (source // Y_LO - my_z + z_count) % z_count
        dy = jnp.where(source % Y_LO == my_y, 0, 1)
        x = normed_s[table_ref[dz * Y_LO + dy] * per_src + in_tile % per_src]
        h = gu_ref[1, m]
        live = (m < cnt_ref[0]).astype(jnp.float32)
        both = jnp.dot(x, gu_v[m], preferred_element_type=jnp.float32) * live
        accg_s[h] += both[:, :tile]
        accu_s[h] += both[:, tile:]
        return carry

    for k, (gate_copy, up_copy) in enumerate(copies):
        gate_copy.wait()
        up_copy.wait()
        lax.fori_loop(k * step, (k + 1) * step, gu_body, 0, unroll=True)
    g = accg_s[...]
    hid_s[...] = (g / (1.0 + jnp.exp(-g)) * accu_s[...]).astype(jnp.bfloat16)
    acco_s[...] = jnp.zeros(acco_s.shape, jnp.float32)

    def dn_body(m, carry):
        o = dn_ref[1, m]
        live = (m < cnt_ref[1]).astype(jnp.float32)
        acco_s[o] += jnp.dot(hid_s[dn_ref[0, m]], d_v[m], preferred_element_type=jnp.float32) * live
        return carry

    for k, down_copy in enumerate(down_copies):
        down_copy.wait()
        lax.fori_loop(k * step, (k + 1) * step, dn_body, 0, unroll=True)
    groups, dests, share, group_width = out_ref.shape
    for h in range(per_src):
        acco_s[me_ref[0] * per_src + h] += piece(0, slice(h * tile, (h + 1) * tile)).astype(jnp.float32)
    per_group = group_width // tile
    for o in range(acco_s.shape[0]):
        block = acco_s[o].reshape(dests, share, tile).astype(out_ref.dtype)
        group, half = divmod(o, per_group)
        out_ref[group, :, :, half * tile:(half + 1) * tile] = block


def ffn(counts, gu_blocks, down_blocks, me, table, pieces, gate_tiles, up_tiles, down_tiles,
        hid_blocks, groups, share):
    layout = []
    for index, array in enumerate(pieces):
        layout += [(index, -1)] if array.ndim == 2 else [(index, sub) for sub in range(array.shape[0])]
    n_src = len(layout)
    rows, width = pieces[0].shape
    tile = gate_tiles.shape[1]
    in_blocks = n_src * width // tile
    smem = pl.BlockSpec(memory_space=pltpu.SMEM)
    vmem = pl.BlockSpec(memory_space=pltpu.VMEM)
    hbm = pl.BlockSpec(memory_space=pl.ANY)
    slots = gate_tiles.shape[0]
    return pl.pallas_call(
        functools.partial(ffn_kernel, tuple(layout)),
        out_shape=jax.ShapeDtypeStruct((groups, rows // share, share, in_blocks * tile // groups),
                                       jnp.bfloat16),
        in_specs=[smem] * 5 + [vmem] * len(pieces) + [hbm] * 3,
        out_specs=vmem,
        scratch_shapes=[
            pltpu.VMEM((in_blocks, rows, tile), jnp.bfloat16),
            pltpu.VMEM((hid_blocks, rows, tile), jnp.float32),
            pltpu.VMEM((hid_blocks, rows, tile), jnp.float32),
            pltpu.VMEM((hid_blocks, rows, tile), jnp.bfloat16),
            pltpu.VMEM((in_blocks, rows, tile), jnp.float32),
            pltpu.VMEM((slots, tile, 2 * tile), jnp.bfloat16),
            pltpu.VMEM((slots, tile, tile), jnp.bfloat16),
            pltpu.SemaphoreType.DMA((3, CHUNKS)),
        ],
    )(counts.reshape(-1), gu_blocks, down_blocks, me.reshape(1), table, *pieces, gate_tiles,
      up_tiles, down_tiles)

def ring_pairs(count, step, flip=0):
    return [(i, ((i // Y_LO + step) % count) * Y_LO + (i % Y_LO ^ flip)) for i in range(count * Y_LO)]


def per_device(tokens, gate_tiles, up_tiles, down_tiles, gu_blocks, down_blocks, counts):
    tp_count = lax.axis_size("tp")
    ctx_count = lax.axis_size("ctx")
    z_count = tp_count // Y_LO
    own_rows, own_width = tokens.shape
    tile = gate_tiles.shape[1]
    per_src = own_width // tile
    me = lax.axis_index("tp")
    my_z = me // Y_LO
    my_y = me % Y_LO
    swap = [(i, i ^ 1) for i in range(tp_count)]
    partner = lax.ppermute(tokens, "tp", swap)
    first = {}
    for step in (1, -1):
        first[step] = (lax.ppermute(tokens, "tp", ring_pairs(z_count, step)),
                       lax.ppermute(tokens, "tp", ring_pairs(z_count, step, 1)))
    partner, first = lax.optimization_barrier((partner, first))
    arrays = [tokens, partner]
    origins = [(0, 0), (0, 1)]
    near = {}
    for step in (1, -1):
        same, other = first[step]
        arrays += [same, other]
        origins += [(-step % z_count, 0), (-step % z_count, 1)]
        near[step] = jnp.stack([same, other])
    far = {}
    for step in (1, -1):
        for hops in (1, 2):
            pair = lax.ppermute(near[step], "tp", ring_pairs(z_count, step * hops))
            arrays.append(pair)
            origins += [(-step * (hops + 1) % z_count, 0), (-step * (hops + 1) % z_count, 1)]
            far[step, hops] = pair
    last = lax.ppermute(far[1, 2], "tp", ring_pairs(z_count, 1))
    arrays.append(last)
    origins += [(-4 % z_count, 0), (-4 % z_count, 1)]
    table = [[0] * Y_LO for _ in range(z_count)]
    for index, (dz, dy) in enumerate(origins):
        table[dz][dy] = index
    feat_width = tp_count * own_width
    hid_blocks = FF // tp_count // tile
    share = own_rows // tp_count
    outgoing = ffn(counts, gu_blocks, down_blocks, me.astype(jnp.int32),
                   jnp.array(table, jnp.int32).reshape(-1), arrays, gate_tiles, up_tiles,
                   down_tiles, hid_blocks, ctx_count, share)
    incoming = lax.all_to_all(
        outgoing.reshape(ctx_count * tp_count, share, feat_width // ctx_count),
        ("ctx", "tp"), 0, 0, tiled=True,
    )
    total = jnp.sum(
        incoming.reshape(ctx_count, tp_count, share, -1).astype(jnp.float32), axis=1
    )
    return jnp.transpose(total, (1, 0, 2)).astype(jnp.bfloat16)


def solution(mesh):
    return jax.shard_map(
        per_device,
        mesh=mesh,
        in_specs=(
            P("ctx", "tp"),
            P("tp", None, None),
            P("tp", None, None),
            P("tp", None, None),
            P(None, "tp"),
            P(None, "tp"),
            P(None, "tp"),
        ),
        out_specs=P("tp", None, "ctx"),
        check_vma=False,
    )
```

```python
import functools

import jax
import jax.numpy as jnp
from jax import lax
from jax.experimental import pallas as pl
from jax.experimental.pallas import tpu as pltpu
from jax.sharding import PartitionSpec as P

FF = 16384
Y_LO = 2
CHUNKS = 8


def ffn_kernel(layout, cnt_ref, gu_ref, dn_ref, me_ref, table_ref, *refs):
    n_src = len(layout)
    n_ops = len(refs) - 12
    piece_refs = refs[:n_ops]
    (g_hbm, u_hbm, d_hbm, out_ref, normed_s, accg_s, accu_s, hid_s, acco_s, gu_v, d_v,
     sems) = refs[n_ops:]
    rows, width = piece_refs[0].shape

    def piece(s, cols):
        ref = piece_refs[layout[s][0]]
        return ref[:, cols] if layout[s][1] < 0 else ref[layout[s][1], :, cols]

    tile = g_hbm.shape[1]
    slots = g_hbm.shape[0]
    step = slots // CHUNKS
    copies = []
    for k in range(CHUNKS):
        part = pl.ds(k * step, step)
        copies.append((
            pltpu.make_async_copy(g_hbm.at[part], gu_v.at[part, :, 0:tile], sems.at[0, k]),
            pltpu.make_async_copy(u_hbm.at[part], gu_v.at[part, :, tile:2 * tile], sems.at[1, k]),
        ))
    down_copies = [
        pltpu.make_async_copy(d_hbm.at[pl.ds(k * step, step)], d_v.at[pl.ds(k * step, step)],
                              sems.at[2, k])
        for k in range(CHUNKS)
    ]
    for gate_copy, up_copy in copies:
        gate_copy.start()
        up_copy.start()
    for down_copy in down_copies:
        down_copy.start()
    per_src = width // tile
    feat = n_src * width
    ss = jnp.zeros((rows, 1), jnp.float32)
    for s in range(n_src):
        x = piece(s, slice(None)).astype(jnp.float32)
        ss = ss + jnp.sum(x * x, axis=1, keepdims=True)
    scale = lax.rsqrt(ss / feat + 1e-05)
    for s in range(n_src):
        for h in range(per_src):
            x = piece(s, slice(h * tile, (h + 1) * tile)).astype(jnp.float32)
            normed_s[s * per_src + h] = (x * scale).astype(jnp.bfloat16)
    accg_s[...] = jnp.zeros(accg_s.shape, jnp.float32)
    accu_s[...] = jnp.zeros(accu_s.shape, jnp.float32)

    z_count = n_src // Y_LO
    my_z = me_ref[0] // Y_LO
    my_y = me_ref[0] % Y_LO

    def gu_body(m, carry):
        in_tile = gu_ref[0, m]
        source = in_tile // per_src
        dz = (source // Y_LO - my_z + z_count) % z_count
        dy = jnp.where(source % Y_LO == my_y, 0, 1)
        x = normed_s[table_ref[dz * Y_LO + dy] * per_src + in_tile % per_src]
        h = gu_ref[1, m]
        live = (m < cnt_ref[0]).astype(jnp.float32)
        both = jnp.dot(x, gu_v[m], preferred_element_type=jnp.float32) * live
        accg_s[h] += both[:, :tile]
        accu_s[h] += both[:, tile:]
        return carry

    for k, (gate_copy, up_copy) in enumerate(copies):
        gate_copy.wait()
        up_copy.wait()
        lax.fori_loop(k * step, (k + 1) * step, gu_body, 0, unroll=True)
    g = accg_s[...]
    hid_s[...] = (g / (1.0 + jnp.exp(-g)) * accu_s[...]).astype(jnp.bfloat16)
    acco_s[...] = jnp.zeros(acco_s.shape, jnp.float32)

    def dn_body(m, carry):
        o = dn_ref[1, m]
        live = (m < cnt_ref[1]).astype(jnp.float32)
        acco_s[o] += jnp.dot(hid_s[dn_ref[0, m]], d_v[m], preferred_element_type=jnp.float32) * live
        return carry

    for k, down_copy in enumerate(down_copies):
        down_copy.wait()
        lax.fori_loop(k * step, (k + 1) * step, dn_body, 0, unroll=True)
    dests, groups, share, group_width = out_ref.shape
    for h in range(per_src):
        acco_s[me_ref[0] * per_src + h] += piece(0, slice(h * tile, (h + 1) * tile)).astype(jnp.float32)
    per_group = group_width // tile
    for o in range(acco_s.shape[0]):
        block = acco_s[o].reshape(dests, share, tile).astype(out_ref.dtype)
        group, half = divmod(o, per_group)
        out_ref[:, group, :, half * tile:(half + 1) * tile] = block


def ffn(counts, gu_blocks, down_blocks, me, table, pieces, gate_tiles, up_tiles, down_tiles,
        hid_blocks, groups, share):
    layout = []
    for index, array in enumerate(pieces):
        layout += [(index, -1)] if array.ndim == 2 else [(index, sub) for sub in range(array.shape[0])]
    n_src = len(layout)
    rows, width = pieces[0].shape
    tile = gate_tiles.shape[1]
    in_blocks = n_src * width // tile
    smem = pl.BlockSpec(memory_space=pltpu.SMEM)
    vmem = pl.BlockSpec(memory_space=pltpu.VMEM)
    hbm = pl.BlockSpec(memory_space=pl.ANY)
    slots = gate_tiles.shape[0]
    return pl.pallas_call(
        functools.partial(ffn_kernel, tuple(layout)),
        out_shape=jax.ShapeDtypeStruct((rows // share, groups, share, in_blocks * tile // groups),
                                       jnp.bfloat16),
        in_specs=[smem] * 5 + [vmem] * len(pieces) + [hbm] * 3,
        out_specs=vmem,
        scratch_shapes=[
            pltpu.VMEM((in_blocks, rows, tile), jnp.bfloat16),
            pltpu.VMEM((hid_blocks, rows, tile), jnp.float32),
            pltpu.VMEM((hid_blocks, rows, tile), jnp.float32),
            pltpu.VMEM((hid_blocks, rows, tile), jnp.bfloat16),
            pltpu.VMEM((in_blocks, rows, tile), jnp.float32),
            pltpu.VMEM((slots, tile, 2 * tile), jnp.bfloat16),
            pltpu.VMEM((slots, tile, tile), jnp.bfloat16),
            pltpu.SemaphoreType.DMA((3, CHUNKS)),
        ],
    )(counts.reshape(-1), gu_blocks, down_blocks, me.reshape(1), table, *pieces, gate_tiles,
      up_tiles, down_tiles)

def ring_pairs(count, step, flip=0):
    return [(i, ((i // Y_LO + step) % count) * Y_LO + (i % Y_LO ^ flip)) for i in range(count * Y_LO)]


def per_device(tokens, gate_tiles, up_tiles, down_tiles, gu_blocks, down_blocks, counts):
    tp_count = lax.axis_size("tp")
    ctx_count = lax.axis_size("ctx")
    z_count = tp_count // Y_LO
    own_rows, own_width = tokens.shape
    tile = gate_tiles.shape[1]
    per_src = own_width // tile
    me = lax.axis_index("tp")
    my_z = me // Y_LO
    my_y = me % Y_LO
    swap = [(i, i ^ 1) for i in range(tp_count)]
    arrays = [tokens, lax.ppermute(tokens, "tp", swap)]
    origins = [(0, 0), (0, 1)]
    near = {}
    for step in (1, -1):
        same = lax.ppermute(tokens, "tp", ring_pairs(z_count, step))
        other = lax.ppermute(tokens, "tp", ring_pairs(z_count, step, 1))
        arrays += [same, other]
        origins += [(-step % z_count, 0), (-step % z_count, 1)]
        near[step] = jnp.stack([same, other])
    far = {}
    for step in (1, -1):
        for hops in (1, 2):
            pair = lax.ppermute(near[step], "tp", ring_pairs(z_count, step * hops))
            arrays.append(pair)
            origins += [(-step * (hops + 1) % z_count, 0), (-step * (hops + 1) % z_count, 1)]
            far[step, hops] = pair
    last = lax.ppermute(far[1, 2], "tp", ring_pairs(z_count, 1))
    arrays.append(last)
    origins += [(-4 % z_count, 0), (-4 % z_count, 1)]
    table = [[0] * Y_LO for _ in range(z_count)]
    for index, (dz, dy) in enumerate(origins):
        table[dz][dy] = index
    feat_width = tp_count * own_width
    hid_blocks = FF // tp_count // tile
    share = own_rows // tp_count
    outgoing = ffn(counts, gu_blocks, down_blocks, me.astype(jnp.int32),
                   jnp.array(table, jnp.int32).reshape(-1), arrays, gate_tiles, up_tiles,
                   down_tiles, hid_blocks, ctx_count, share)
    incoming = lax.all_to_all(
        outgoing.reshape(ctx_count * tp_count, share, feat_width // ctx_count),
        ("tp", "ctx"), 0, 0, tiled=True,
    )
    total = jnp.sum(
        incoming.reshape(tp_count, ctx_count, share, -1).astype(jnp.float32), axis=0
    )
    return jnp.transpose(total, (1, 0, 2)).astype(jnp.bfloat16)


def solution(mesh):
    return jax.shard_map(
        per_device,
        mesh=mesh,
        in_specs=(
            P("ctx", "tp"),
            P("tp", None, None),
            P("tp", None, None),
            P("tp", None, None),
            P(None, "tp"),
            P(None, "tp"),
            P(None, "tp"),
        ),
        out_specs=P("tp", None, "ctx"),
        check_vma=False,
    )
```

```python
import functools

import jax
import jax.numpy as jnp
from jax import lax
from jax.experimental import pallas as pl
from jax.experimental.pallas import tpu as pltpu
from jax.sharding import PartitionSpec as P

FF = 16384
Y_LO = 2
CHUNKS = 8


def ffn_kernel(layout, cnt_ref, gu_ref, dn_ref, me_ref, table_ref, *refs):
    n_src = len(layout)
    n_ops = len(refs) - 12
    piece_refs = refs[:n_ops]
    (g_hbm, u_hbm, d_hbm, out_ref, normed_s, accg_s, accu_s, hid_s, acco_s, gu_v, d_v,
     sems) = refs[n_ops:]
    rows, width = piece_refs[0].shape

    def piece(s, cols):
        ref = piece_refs[layout[s][0]]
        return ref[:, cols] if layout[s][1] < 0 else ref[layout[s][1], :, cols]

    tile = g_hbm.shape[1]
    slots = g_hbm.shape[0]
    step = slots // CHUNKS
    copies = []
    for k in range(CHUNKS):
        part = pl.ds(k * step, step)
        copies.append((
            pltpu.make_async_copy(g_hbm.at[part], gu_v.at[part, :, 0:tile], sems.at[0, k]),
            pltpu.make_async_copy(u_hbm.at[part], gu_v.at[part, :, tile:2 * tile], sems.at[1, k]),
        ))
    down_copies = [
        pltpu.make_async_copy(d_hbm.at[pl.ds(k * step, step)], d_v.at[pl.ds(k * step, step)],
                              sems.at[2, k])
        for k in range(CHUNKS)
    ]
    for gate_copy, up_copy in copies:
        gate_copy.start()
        up_copy.start()
    for down_copy in down_copies:
        down_copy.start()
    per_src = width // tile
    feat = n_src * width
    ss = jnp.zeros((rows, 1), jnp.float32)
    for s in range(n_src):
        x = piece(s, slice(None)).astype(jnp.float32)
        ss = ss + jnp.sum(x * x, axis=1, keepdims=True)
    scale = lax.rsqrt(ss / feat + 1e-05)
    for s in range(n_src):
        for h in range(per_src):
            x = piece(s, slice(h * tile, (h + 1) * tile)).astype(jnp.float32)
            normed_s[s * per_src + h] = (x * scale).astype(jnp.bfloat16)
    accg_s[...] = jnp.zeros(accg_s.shape, jnp.float32)
    accu_s[...] = jnp.zeros(accu_s.shape, jnp.float32)

    z_count = n_src // Y_LO
    my_z = me_ref[0] // Y_LO
    my_y = me_ref[0] % Y_LO

    def gu_body(m, carry):
        in_tile = gu_ref[0, m]
        source = in_tile // per_src
        dz = (source // Y_LO - my_z + z_count) % z_count
        dy = jnp.where(source % Y_LO == my_y, 0, 1)
        x = normed_s[table_ref[dz * Y_LO + dy] * per_src + in_tile % per_src]
        h = gu_ref[1, m]
        live = (m < cnt_ref[0]).astype(jnp.float32)
        both = jnp.dot(x, gu_v[m], preferred_element_type=jnp.float32) * live
        accg_s[h] += both[:, :tile]
        accu_s[h] += both[:, tile:]
        return carry

    for k, (gate_copy, up_copy) in enumerate(copies):
        gate_copy.wait()
        up_copy.wait()
        lax.fori_loop(k * step, (k + 1) * step, gu_body, 0, unroll=True)
    g = accg_s[...]
    hid_s[...] = (g / (1.0 + jnp.exp(-g)) * accu_s[...]).astype(jnp.bfloat16)
    acco_s[...] = jnp.zeros(acco_s.shape, jnp.float32)

    def dn_body(m, carry):
        o = dn_ref[1, m]
        live = (m < cnt_ref[1]).astype(jnp.float32)
        acco_s[o] += jnp.dot(hid_s[dn_ref[0, m]], d_v[m], preferred_element_type=jnp.float32) * live
        return carry

    for k, down_copy in enumerate(down_copies):
        down_copy.wait()
        lax.fori_loop(k * step, (k + 1) * step, dn_body, 0, unroll=True)
    groups, dests, share, group_width = out_ref.shape
    for h in range(per_src):
        acco_s[me_ref[0] * per_src + h] += piece(0, slice(h * tile, (h + 1) * tile)).astype(jnp.float32)
    per_group = group_width // tile
    for o in range(acco_s.shape[0]):
        block = acco_s[o].reshape(dests, share, tile).astype(out_ref.dtype)
        group, half = divmod(o, per_group)
        out_ref[group, :, :, half * tile:(half + 1) * tile] = block


def ffn(counts, gu_blocks, down_blocks, me, table, pieces, gate_tiles, up_tiles, down_tiles,
        hid_blocks, groups, share):
    layout = []
    for index, array in enumerate(pieces):
        layout += [(index, -1)] if array.ndim == 2 else [(index, sub) for sub in range(array.shape[0])]
    n_src = len(layout)
    rows, width = pieces[0].shape
    tile = gate_tiles.shape[1]
    in_blocks = n_src * width // tile
    smem = pl.BlockSpec(memory_space=pltpu.SMEM)
    vmem = pl.BlockSpec(memory_space=pltpu.VMEM)
    hbm = pl.BlockSpec(memory_space=pl.ANY)
    slots = gate_tiles.shape[0]
    return pl.pallas_call(
        functools.partial(ffn_kernel, tuple(layout)),
        out_shape=jax.ShapeDtypeStruct((groups, rows // share, share, in_blocks * tile // groups),
                                       jnp.bfloat16),
        in_specs=[smem] * 5 + [vmem] * len(pieces) + [hbm] * 3,
        out_specs=vmem,
        scratch_shapes=[
            pltpu.VMEM((in_blocks, rows, tile), jnp.bfloat16),
            pltpu.VMEM((hid_blocks, rows, tile), jnp.float32),
            pltpu.VMEM((hid_blocks, rows, tile), jnp.float32),
            pltpu.VMEM((hid_blocks, rows, tile), jnp.bfloat16),
            pltpu.VMEM((in_blocks, rows, tile), jnp.float32),
            pltpu.VMEM((slots, tile, 2 * tile), jnp.bfloat16),
            pltpu.VMEM((slots, tile, tile), jnp.bfloat16),
            pltpu.SemaphoreType.DMA((3, CHUNKS)),
        ],
    )(counts.reshape(-1), gu_blocks, down_blocks, me.reshape(1), table, *pieces, gate_tiles,
      up_tiles, down_tiles)

def ring_pairs(count, step, flip=0):
    return [(i, ((i // Y_LO + step) % count) * Y_LO + (i % Y_LO ^ flip)) for i in range(count * Y_LO)]


def per_device(tokens, gate_tiles, up_tiles, down_tiles, gu_blocks, down_blocks, counts):
    tp_count = lax.axis_size("tp")
    ctx_count = lax.axis_size("ctx")
    z_count = tp_count // Y_LO
    own_rows, own_width = tokens.shape
    tile = gate_tiles.shape[1]
    per_src = own_width // tile
    me = lax.axis_index("tp")
    my_z = me // Y_LO
    my_y = me % Y_LO
    arrays = [tokens]
    origins = [(0, 0)]
    near = {}
    for step in (1, -1):
        same = lax.ppermute(tokens, "tp", ring_pairs(z_count, step))
        other = lax.ppermute(tokens, "tp", ring_pairs(z_count, step, 1))
        arrays += [same, other]
        origins += [(-step % z_count, 0), (-step % z_count, 1)]
        near[step] = (same, other)
    far = {}
    for step in (1, -1):
        for hops in (1, 2):
            carried = list(near[step])
            if step == 1 and hops == 1:
                carried.append(near[-1][1])
            pair = lax.ppermute(jnp.stack(carried), "tp", ring_pairs(z_count, step * hops))
            arrays.append(pair)
            origins += [(-step * (hops + 1) % z_count, 0), (-step * (hops + 1) % z_count, 1)]
            if step == 1 and hops == 1:
                origins.append((0, 1))
            far[step, hops] = pair
    last = lax.ppermute(far[1, 2], "tp", ring_pairs(z_count, 1))
    arrays.append(last)
    origins += [(-4 % z_count, 0), (-4 % z_count, 1)]
    table = [[0] * Y_LO for _ in range(z_count)]
    for index, (dz, dy) in enumerate(origins):
        table[dz][dy] = index
    feat_width = tp_count * own_width
    hid_blocks = FF // tp_count // tile
    share = own_rows // tp_count
    outgoing = ffn(counts, gu_blocks, down_blocks, me.astype(jnp.int32),
                   jnp.array(table, jnp.int32).reshape(-1), arrays, gate_tiles, up_tiles,
                   down_tiles, hid_blocks, ctx_count, share)
    incoming = lax.all_to_all(
        outgoing.reshape(ctx_count * tp_count, share, feat_width // ctx_count),
        ("ctx", "tp"), 0, 0, tiled=True,
    )
    total = jnp.sum(
        incoming.reshape(ctx_count, tp_count, share, -1).astype(jnp.float32), axis=1
    )
    return jnp.transpose(total, (1, 0, 2)).astype(jnp.bfloat16)


def solution(mesh):
    return jax.shard_map(
        per_device,
        mesh=mesh,
        in_specs=(
            P("ctx", "tp"),
            P("tp", None, None),
            P("tp", None, None),
            P("tp", None, None),
            P(None, "tp"),
            P(None, "tp"),
            P(None, "tp"),
        ),
        out_specs=P("tp", None, "ctx"),
        check_vma=False,
    )
```

```python
import functools

import jax
import jax.numpy as jnp
from jax import lax
from jax.experimental import pallas as pl
from jax.experimental.pallas import tpu as pltpu
from jax.sharding import PartitionSpec as P

FF = 16384
Y_LO = 2
CHUNKS = 8


def ffn_kernel(layout, cnt_ref, gu_ref, dn_ref, me_ref, table_ref, *refs):
    n_src = len(layout)
    n_ops = len(refs) - 14
    piece_refs = refs[:n_ops]
    (g_hbm, u_hbm, d_hbm, out_ref, normed_s, accg_s, accu_s, hid_s, acco_s, gu_v, d_v,
     sems, pieces_v, piece_sems) = refs[n_ops:]
    rows, width = pieces_v.shape[1:]
    arrivals = []
    for index, ref in enumerate(piece_refs):
        first = [s for s in range(n_src) if layout[s][0] == index][0]
        count = 1 if len(ref.shape) == 2 else ref.shape[0]
        target = pieces_v.at[first] if len(ref.shape) == 2 else pieces_v.at[pl.ds(first, count)]
        arrivals.append(pltpu.make_async_copy(ref, target, piece_sems.at[index]))
    for arrival in arrivals:
        arrival.start()

    def piece(s, cols):
        return pieces_v[s, :, cols]

    tile = g_hbm.shape[1]
    slots = g_hbm.shape[0]
    step = slots // CHUNKS
    copies = []
    for k in range(CHUNKS):
        part = pl.ds(k * step, step)
        copies.append((
            pltpu.make_async_copy(g_hbm.at[part], gu_v.at[part, :, 0:tile], sems.at[0, k]),
            pltpu.make_async_copy(u_hbm.at[part], gu_v.at[part, :, tile:2 * tile], sems.at[1, k]),
        ))
    down_copies = [
        pltpu.make_async_copy(d_hbm.at[pl.ds(k * step, step)], d_v.at[pl.ds(k * step, step)],
                              sems.at[2, k])
        for k in range(CHUNKS)
    ]
    for gate_copy, up_copy in copies:
        gate_copy.start()
        up_copy.start()
    for down_copy in down_copies:
        down_copy.start()
    per_src = width // tile
    feat = n_src * width
    for arrival in arrivals:
        arrival.wait()
    ss = jnp.zeros((rows, 1), jnp.float32)
    for s in range(n_src):
        x = piece(s, slice(None)).astype(jnp.float32)
        ss = ss + jnp.sum(x * x, axis=1, keepdims=True)
    scale = lax.rsqrt(ss / feat + 1e-05)
    for s in range(n_src):
        for h in range(per_src):
            x = piece(s, slice(h * tile, (h + 1) * tile)).astype(jnp.float32)
            normed_s[s * per_src + h] = (x * scale).astype(jnp.bfloat16)
    accg_s[...] = jnp.zeros(accg_s.shape, jnp.float32)
    accu_s[...] = jnp.zeros(accu_s.shape, jnp.float32)

    z_count = n_src // Y_LO
    my_z = me_ref[0] // Y_LO
    my_y = me_ref[0] % Y_LO

    def gu_body(m, carry):
        in_tile = gu_ref[0, m]
        source = in_tile // per_src
        dz = (source // Y_LO - my_z + z_count) % z_count
        dy = jnp.where(source % Y_LO == my_y, 0, 1)
        x = normed_s[table_ref[dz * Y_LO + dy] * per_src + in_tile % per_src]
        h = gu_ref[1, m]
        live = (m < cnt_ref[0]).astype(jnp.float32)
        both = jnp.dot(x, gu_v[m], preferred_element_type=jnp.float32) * live
        accg_s[h] += both[:, :tile]
        accu_s[h] += both[:, tile:]
        return carry

    for k, (gate_copy, up_copy) in enumerate(copies):
        gate_copy.wait()
        up_copy.wait()
        lax.fori_loop(k * step, (k + 1) * step, gu_body, 0, unroll=True)
    g = accg_s[...]
    hid_s[...] = (g / (1.0 + jnp.exp(-g)) * accu_s[...]).astype(jnp.bfloat16)
    acco_s[...] = jnp.zeros(acco_s.shape, jnp.float32)

    def dn_body(m, carry):
        o = dn_ref[1, m]
        live = (m < cnt_ref[1]).astype(jnp.float32)
        acco_s[o] += jnp.dot(hid_s[dn_ref[0, m]], d_v[m], preferred_element_type=jnp.float32) * live
        return carry

    for k, down_copy in enumerate(down_copies):
        down_copy.wait()
        lax.fori_loop(k * step, (k + 1) * step, dn_body, 0, unroll=True)
    groups, dests, share, group_width = out_ref.shape
    for h in range(per_src):
        acco_s[me_ref[0] * per_src + h] += piece(0, slice(h * tile, (h + 1) * tile)).astype(jnp.float32)
    per_group = group_width // tile
    for o in range(acco_s.shape[0]):
        block = acco_s[o].reshape(dests, share, tile).astype(out_ref.dtype)
        group, half = divmod(o, per_group)
        out_ref[group, :, :, half * tile:(half + 1) * tile] = block


def ffn(counts, gu_blocks, down_blocks, me, table, pieces, gate_tiles, up_tiles, down_tiles,
        hid_blocks, groups, share):
    layout = []
    for index, array in enumerate(pieces):
        layout += [(index, -1)] if array.ndim == 2 else [(index, sub) for sub in range(array.shape[0])]
    n_src = len(layout)
    rows, width = pieces[0].shape
    tile = gate_tiles.shape[1]
    in_blocks = n_src * width // tile
    smem = pl.BlockSpec(memory_space=pltpu.SMEM)
    vmem = pl.BlockSpec(memory_space=pltpu.VMEM)
    hbm = pl.BlockSpec(memory_space=pl.ANY)
    slots = gate_tiles.shape[0]
    return pl.pallas_call(
        functools.partial(ffn_kernel, tuple(layout)),
        out_shape=jax.ShapeDtypeStruct((groups, rows // share, share, in_blocks * tile // groups),
                                       jnp.bfloat16),
        in_specs=[smem] * 5 + [hbm] * len(pieces) + [hbm] * 3,
        out_specs=vmem,
        scratch_shapes=[
            pltpu.VMEM((in_blocks, rows, tile), jnp.bfloat16),
            pltpu.VMEM((hid_blocks, rows, tile), jnp.float32),
            pltpu.VMEM((hid_blocks, rows, tile), jnp.float32),
            pltpu.VMEM((hid_blocks, rows, tile), jnp.bfloat16),
            pltpu.VMEM((in_blocks, rows, tile), jnp.float32),
            pltpu.VMEM((slots, tile, 2 * tile), jnp.bfloat16),
            pltpu.VMEM((slots, tile, tile), jnp.bfloat16),
            pltpu.SemaphoreType.DMA((3, CHUNKS)),
            pltpu.VMEM((n_src, rows, width), jnp.bfloat16),
            pltpu.SemaphoreType.DMA((len(pieces),)),
        ],
    )(counts.reshape(-1), gu_blocks, down_blocks, me.reshape(1), table, *pieces, gate_tiles,
      up_tiles, down_tiles)

def ring_pairs(count, step, flip=0):
    return [(i, ((i // Y_LO + step) % count) * Y_LO + (i % Y_LO ^ flip)) for i in range(count * Y_LO)]


def per_device(tokens, gate_tiles, up_tiles, down_tiles, gu_blocks, down_blocks, counts):
    tp_count = lax.axis_size("tp")
    ctx_count = lax.axis_size("ctx")
    z_count = tp_count // Y_LO
    own_rows, own_width = tokens.shape
    tile = gate_tiles.shape[1]
    per_src = own_width // tile
    me = lax.axis_index("tp")
    my_z = me // Y_LO
    my_y = me % Y_LO
    swap = [(i, i ^ 1) for i in range(tp_count)]
    arrays = [tokens, lax.ppermute(tokens, "tp", swap)]
    origins = [(0, 0), (0, 1)]
    near = {}
    for step in (1, -1):
        same = lax.ppermute(tokens, "tp", ring_pairs(z_count, step))
        other = lax.ppermute(tokens, "tp", ring_pairs(z_count, step, 1))
        arrays += [same, other]
        origins += [(-step % z_count, 0), (-step % z_count, 1)]
        near[step] = jnp.stack([same, other])
    far = {}
    for step in (1, -1):
        for hops in (1, 2):
            pair = lax.ppermute(near[step], "tp", ring_pairs(z_count, step * hops))
            arrays.append(pair)
            origins += [(-step * (hops + 1) % z_count, 0), (-step * (hops + 1) % z_count, 1)]
            far[step, hops] = pair
    last = lax.ppermute(far[1, 2], "tp", ring_pairs(z_count, 1))
    arrays.append(last)
    origins += [(-4 % z_count, 0), (-4 % z_count, 1)]
    table = [[0] * Y_LO for _ in range(z_count)]
    for index, (dz, dy) in enumerate(origins):
        table[dz][dy] = index
    feat_width = tp_count * own_width
    hid_blocks = FF // tp_count // tile
    share = own_rows // tp_count
    outgoing = ffn(counts, gu_blocks, down_blocks, me.astype(jnp.int32),
                   jnp.array(table, jnp.int32).reshape(-1), arrays, gate_tiles, up_tiles,
                   down_tiles, hid_blocks, ctx_count, share)
    incoming = lax.all_to_all(
        outgoing.reshape(ctx_count * tp_count, share, feat_width // ctx_count),
        ("ctx", "tp"), 0, 0, tiled=True,
    )
    total = jnp.sum(
        incoming.reshape(ctx_count, tp_count, share, -1).astype(jnp.float32), axis=1
    )
    return jnp.transpose(total, (1, 0, 2)).astype(jnp.bfloat16)


def solution(mesh):
    return jax.shard_map(
        per_device,
        mesh=mesh,
        in_specs=(
            P("ctx", "tp"),
            P("tp", None, None),
            P("tp", None, None),
            P("tp", None, None),
            P(None, "tp"),
            P(None, "tp"),
            P(None, "tp"),
        ),
        out_specs=P("tp", None, "ctx"),
        check_vma=False,
    )
```

```python
import functools

import jax
import jax.numpy as jnp
from jax import lax
from jax.experimental import pallas as pl
from jax.experimental.pallas import tpu as pltpu
from jax.sharding import PartitionSpec as P

FF = 16384
Y_LO = 2
CHUNKS = 2


def ffn_kernel(layout, cnt_ref, gu_ref, dn_ref, me_ref, table_ref, *refs):
    n_src = len(layout)
    n_ops = len(refs) - 12
    piece_refs = refs[:n_ops]
    (g_hbm, u_hbm, d_hbm, out_ref, normed_s, accg_s, accu_s, hid_s, acco_s, gu_v, d_v,
     sems) = refs[n_ops:]
    rows, width = piece_refs[0].shape

    def piece(s, cols):
        ref = piece_refs[layout[s][0]]
        return ref[:, cols] if layout[s][1] < 0 else ref[layout[s][1], :, cols]

    tile = g_hbm.shape[1]
    slots = g_hbm.shape[0]
    step = slots // CHUNKS
    copies = []
    for k in range(CHUNKS):
        part = pl.ds(k * step, step)
        copies.append((
            pltpu.make_async_copy(g_hbm.at[part], gu_v.at[part, :, 0:tile], sems.at[0, k]),
            pltpu.make_async_copy(u_hbm.at[part], gu_v.at[part, :, tile:2 * tile], sems.at[1, k]),
        ))
    down_copies = [
        pltpu.make_async_copy(d_hbm.at[pl.ds(k * step, step)], d_v.at[pl.ds(k * step, step)],
                              sems.at[2, k])
        for k in range(CHUNKS)
    ]
    for gate_copy, up_copy in copies:
        gate_copy.start()
        up_copy.start()
    for down_copy in down_copies:
        down_copy.start()
    per_src = width // tile
    feat = n_src * width
    ss = jnp.zeros((rows, 1), jnp.float32)
    for s in range(n_src):
        x = piece(s, slice(None)).astype(jnp.float32)
        ss = ss + jnp.sum(x * x, axis=1, keepdims=True)
    scale = lax.rsqrt(ss / feat + 1e-05)
    for s in range(n_src):
        for h in range(per_src):
            x = piece(s, slice(h * tile, (h + 1) * tile)).astype(jnp.float32)
            normed_s[s * per_src + h] = (x * scale).astype(jnp.bfloat16)
    accg_s[...] = jnp.zeros(accg_s.shape, jnp.float32)
    accu_s[...] = jnp.zeros(accu_s.shape, jnp.float32)

    z_count = n_src // Y_LO
    my_z = me_ref[0] // Y_LO
    my_y = me_ref[0] % Y_LO

    def gu_body(m, carry):
        in_tile = gu_ref[0, m]
        source = in_tile // per_src
        dz = (source // Y_LO - my_z + z_count) % z_count
        dy = jnp.where(source % Y_LO == my_y, 0, 1)
        x = normed_s[table_ref[dz * Y_LO + dy] * per_src + in_tile % per_src]
        h = gu_ref[1, m]
        live = (m < cnt_ref[0]).astype(jnp.float32)
        both = jnp.dot(x, gu_v[m], preferred_element_type=jnp.float32) * live
        accg_s[h] += both[:, :tile]
        accu_s[h] += both[:, tile:]
        return carry

    for k, (gate_copy, up_copy) in enumerate(copies):
        gate_copy.wait()
        up_copy.wait()
        lax.fori_loop(k * step, (k + 1) * step, gu_body, 0, unroll=True)
    g = accg_s[...]
    hid_s[...] = (g / (1.0 + jnp.exp(-g)) * accu_s[...]).astype(jnp.bfloat16)
    acco_s[...] = jnp.zeros(acco_s.shape, jnp.float32)

    def dn_body(m, carry):
        o = dn_ref[1, m]
        live = (m < cnt_ref[1]).astype(jnp.float32)
        acco_s[o] += jnp.dot(hid_s[dn_ref[0, m]], d_v[m], preferred_element_type=jnp.float32) * live
        return carry

    for k, down_copy in enumerate(down_copies):
        down_copy.wait()
        lax.fori_loop(k * step, (k + 1) * step, dn_body, 0, unroll=True)
    groups, dests, share, group_width = out_ref.shape
    for h in range(per_src):
        acco_s[me_ref[0] * per_src + h] += piece(0, slice(h * tile, (h + 1) * tile)).astype(jnp.float32)
    per_group = group_width // tile
    for o in range(acco_s.shape[0]):
        block = acco_s[o].reshape(dests, share, tile).astype(out_ref.dtype)
        group, half = divmod(o, per_group)
        out_ref[group, :, :, half * tile:(half + 1) * tile] = block


def ffn(counts, gu_blocks, down_blocks, me, table, pieces, gate_tiles, up_tiles, down_tiles,
        hid_blocks, groups, share):
    layout = []
    for index, array in enumerate(pieces):
        layout += [(index, -1)] if array.ndim == 2 else [(index, sub) for sub in range(array.shape[0])]
    n_src = len(layout)
    rows, width = pieces[0].shape
    tile = gate_tiles.shape[1]
    in_blocks = n_src * width // tile
    smem = pl.BlockSpec(memory_space=pltpu.SMEM)
    vmem = pl.BlockSpec(memory_space=pltpu.VMEM)
    hbm = pl.BlockSpec(memory_space=pl.ANY)
    slots = gate_tiles.shape[0]
    return pl.pallas_call(
        functools.partial(ffn_kernel, tuple(layout)),
        out_shape=jax.ShapeDtypeStruct((groups, rows // share, share, in_blocks * tile // groups),
                                       jnp.bfloat16),
        in_specs=[smem] * 5 + [vmem] * len(pieces) + [hbm] * 3,
        out_specs=vmem,
        scratch_shapes=[
            pltpu.VMEM((in_blocks, rows, tile), jnp.bfloat16),
            pltpu.VMEM((hid_blocks, rows, tile), jnp.float32),
            pltpu.VMEM((hid_blocks, rows, tile), jnp.float32),
            pltpu.VMEM((hid_blocks, rows, tile), jnp.bfloat16),
            pltpu.VMEM((in_blocks, rows, tile), jnp.float32),
            pltpu.VMEM((slots, tile, 2 * tile), jnp.bfloat16),
            pltpu.VMEM((slots, tile, tile), jnp.bfloat16),
            pltpu.SemaphoreType.DMA((3, CHUNKS)),
        ],
    )(counts.reshape(-1), gu_blocks, down_blocks, me.reshape(1), table, *pieces, gate_tiles,
      up_tiles, down_tiles)

def ring_pairs(count, step, flip=0):
    return [(i, ((i // Y_LO + step) % count) * Y_LO + (i % Y_LO ^ flip)) for i in range(count * Y_LO)]


def per_device(tokens, gate_tiles, up_tiles, down_tiles, gu_blocks, down_blocks, counts):
    tp_count = lax.axis_size("tp")
    ctx_count = lax.axis_size("ctx")
    z_count = tp_count // Y_LO
    own_rows, own_width = tokens.shape
    tile = gate_tiles.shape[1]
    per_src = own_width // tile
    me = lax.axis_index("tp")
    my_z = me // Y_LO
    my_y = me % Y_LO
    swap = [(i, i ^ 1) for i in range(tp_count)]
    arrays = [tokens, lax.ppermute(tokens, "tp", swap)]
    origins = [(0, 0), (0, 1)]
    near = {}
    for step in (1, -1):
        same = lax.ppermute(tokens, "tp", ring_pairs(z_count, step))
        other = lax.ppermute(tokens, "tp", ring_pairs(z_count, step, 1))
        arrays += [same, other]
        origins += [(-step % z_count, 0), (-step % z_count, 1)]
        near[step] = jnp.stack([same, other])
    far = {}
    for step in (1, -1):
        for hops in (1, 2):
            pair = lax.ppermute(near[step], "tp", ring_pairs(z_count, step * hops))
            arrays.append(pair)
            origins += [(-step * (hops + 1) % z_count, 0), (-step * (hops + 1) % z_count, 1)]
            far[step, hops] = pair
    last = lax.ppermute(far[1, 2], "tp", ring_pairs(z_count, 1))
    arrays.append(last)
    origins += [(-4 % z_count, 0), (-4 % z_count, 1)]
    table = [[0] * Y_LO for _ in range(z_count)]
    for index, (dz, dy) in enumerate(origins):
        table[dz][dy] = index
    feat_width = tp_count * own_width
    hid_blocks = FF // tp_count // tile
    share = own_rows // tp_count
    outgoing = ffn(counts, gu_blocks, down_blocks, me.astype(jnp.int32),
                   jnp.array(table, jnp.int32).reshape(-1), arrays, gate_tiles, up_tiles,
                   down_tiles, hid_blocks, ctx_count, share)
    incoming = lax.all_to_all(
        outgoing.reshape(ctx_count * tp_count, share, feat_width // ctx_count),
        ("ctx", "tp"), 0, 0, tiled=True,
    )
    total = jnp.sum(
        incoming.reshape(ctx_count, tp_count, share, -1).astype(jnp.float32), axis=1
    )
    return jnp.transpose(total, (1, 0, 2)).astype(jnp.bfloat16)


def solution(mesh):
    return jax.shard_map(
        per_device,
        mesh=mesh,
        in_specs=(
            P("ctx", "tp"),
            P("tp", None, None),
            P("tp", None, None),
            P("tp", None, None),
            P(None, "tp"),
            P(None, "tp"),
            P(None, "tp"),
        ),
        out_specs=P("tp", None, "ctx"),
        check_vma=False,
    )
```

```python
import functools

import jax
import jax.numpy as jnp
from jax import lax
from jax.experimental import pallas as pl
from jax.experimental.pallas import tpu as pltpu
from jax.sharding import PartitionSpec as P

FF = 16384
Y_LO = 2
CHUNKS = 2


def ffn_kernel(layout, cnt_ref, gu_ref, dn_ref, me_ref, table_ref, *refs):
    n_src = len(layout)
    n_ops = len(refs) - 12
    piece_refs = refs[:n_ops]
    (g_hbm, u_hbm, d_hbm, out_ref, normed_s, accg_s, accu_s, hid_s, acco_s, gu_v, d_v,
     sems) = refs[n_ops:]
    rows, width = piece_refs[0].shape

    def piece(s, cols):
        ref = piece_refs[layout[s][0]]
        return ref[:, cols] if layout[s][1] < 0 else ref[layout[s][1], :, cols]

    tile = g_hbm.shape[1]
    slots = g_hbm.shape[0]
    step = slots // CHUNKS
    copies = []
    for k in range(CHUNKS):
        part = pl.ds(k * step, step)
        copies.append((
            pltpu.make_async_copy(g_hbm.at[part], gu_v.at[part, :, 0:tile], sems.at[0, k]),
            pltpu.make_async_copy(u_hbm.at[part], gu_v.at[part, :, tile:2 * tile], sems.at[1, k]),
        ))
    down_copies = [pltpu.make_async_copy(d_hbm, d_v, sems.at[2, 0])]
    for gate_copy, up_copy in copies:
        gate_copy.start()
        up_copy.start()
    for down_copy in down_copies:
        down_copy.start()
    per_src = width // tile
    feat = n_src * width
    ss = jnp.zeros((rows, 1), jnp.float32)
    for s in range(n_src):
        x = piece(s, slice(None)).astype(jnp.float32)
        ss = ss + jnp.sum(x * x, axis=1, keepdims=True)
    scale = lax.rsqrt(ss / feat + 1e-05)
    for s in range(n_src):
        for h in range(per_src):
            x = piece(s, slice(h * tile, (h + 1) * tile)).astype(jnp.float32)
            normed_s[s * per_src + h] = (x * scale).astype(jnp.bfloat16)
    accg_s[...] = jnp.zeros(accg_s.shape, jnp.float32)
    accu_s[...] = jnp.zeros(accu_s.shape, jnp.float32)

    z_count = n_src // Y_LO
    my_z = me_ref[0] // Y_LO
    my_y = me_ref[0] % Y_LO

    def gu_body(m, carry):
        in_tile = gu_ref[0, m]
        source = in_tile // per_src
        dz = (source // Y_LO - my_z + z_count) % z_count
        dy = jnp.where(source % Y_LO == my_y, 0, 1)
        x = normed_s[table_ref[dz * Y_LO + dy] * per_src + in_tile % per_src]
        h = gu_ref[1, m]
        live = (m < cnt_ref[0]).astype(jnp.float32)
        both = jnp.dot(x, gu_v[m], preferred_element_type=jnp.float32) * live
        accg_s[h] += both[:, :tile]
        accu_s[h] += both[:, tile:]
        return carry

    for k, (gate_copy, up_copy) in enumerate(copies):
        gate_copy.wait()
        up_copy.wait()
        lax.fori_loop(k * step, (k + 1) * step, gu_body, 0, unroll=True)
    g = accg_s[...]
    hid_s[...] = (g / (1.0 + jnp.exp(-g)) * accu_s[...]).astype(jnp.bfloat16)
    acco_s[...] = jnp.zeros(acco_s.shape, jnp.float32)

    def dn_body(m, carry):
        o = dn_ref[1, m]
        live = (m < cnt_ref[1]).astype(jnp.float32)
        acco_s[o] += jnp.dot(hid_s[dn_ref[0, m]], d_v[m], preferred_element_type=jnp.float32) * live
        return carry

    for k, down_copy in enumerate(down_copies):
        down_copy.wait()
        lax.fori_loop(0, slots, dn_body, 0, unroll=True)
    groups, dests, share, group_width = out_ref.shape
    for h in range(per_src):
        acco_s[me_ref[0] * per_src + h] += piece(0, slice(h * tile, (h + 1) * tile)).astype(jnp.float32)
    per_group = group_width // tile
    for o in range(acco_s.shape[0]):
        block = acco_s[o].reshape(dests, share, tile).astype(out_ref.dtype)
        group, half = divmod(o, per_group)
        out_ref[group, :, :, half * tile:(half + 1) * tile] = block


def ffn(counts, gu_blocks, down_blocks, me, table, pieces, gate_tiles, up_tiles, down_tiles,
        hid_blocks, groups, share):
    layout = []
    for index, array in enumerate(pieces):
        layout += [(index, -1)] if array.ndim == 2 else [(index, sub) for sub in range(array.shape[0])]
    n_src = len(layout)
    rows, width = pieces[0].shape
    tile = gate_tiles.shape[1]
    in_blocks = n_src * width // tile
    smem = pl.BlockSpec(memory_space=pltpu.SMEM)
    vmem = pl.BlockSpec(memory_space=pltpu.VMEM)
    hbm = pl.BlockSpec(memory_space=pl.ANY)
    slots = gate_tiles.shape[0]
    return pl.pallas_call(
        functools.partial(ffn_kernel, tuple(layout)),
        out_shape=jax.ShapeDtypeStruct((groups, rows // share, share, in_blocks * tile // groups),
                                       jnp.bfloat16),
        in_specs=[smem] * 5 + [vmem] * len(pieces) + [hbm] * 3,
        out_specs=vmem,
        scratch_shapes=[
            pltpu.VMEM((in_blocks, rows, tile), jnp.bfloat16),
            pltpu.VMEM((hid_blocks, rows, tile), jnp.float32),
            pltpu.VMEM((hid_blocks, rows, tile), jnp.float32),
            pltpu.VMEM((hid_blocks, rows, tile), jnp.bfloat16),
            pltpu.VMEM((in_blocks, rows, tile), jnp.float32),
            pltpu.VMEM((slots, tile, 2 * tile), jnp.bfloat16),
            pltpu.VMEM((slots, tile, tile), jnp.bfloat16),
            pltpu.SemaphoreType.DMA((3, CHUNKS)),
        ],
    )(counts.reshape(-1), gu_blocks, down_blocks, me.reshape(1), table, *pieces, gate_tiles,
      up_tiles, down_tiles)

def ring_pairs(count, step, flip=0):
    return [(i, ((i // Y_LO + step) % count) * Y_LO + (i % Y_LO ^ flip)) for i in range(count * Y_LO)]


def per_device(tokens, gate_tiles, up_tiles, down_tiles, gu_blocks, down_blocks, counts):
    tp_count = lax.axis_size("tp")
    ctx_count = lax.axis_size("ctx")
    z_count = tp_count // Y_LO
    own_rows, own_width = tokens.shape
    tile = gate_tiles.shape[1]
    per_src = own_width // tile
    me = lax.axis_index("tp")
    my_z = me // Y_LO
    my_y = me % Y_LO
    swap = [(i, i ^ 1) for i in range(tp_count)]
    arrays = [tokens, lax.ppermute(tokens, "tp", swap)]
    origins = [(0, 0), (0, 1)]
    near = {}
    for step in (1, -1):
        same = lax.ppermute(tokens, "tp", ring_pairs(z_count, step))
        other = lax.ppermute(tokens, "tp", ring_pairs(z_count, step, 1))
        arrays += [same, other]
        origins += [(-step % z_count, 0), (-step % z_count, 1)]
        near[step] = jnp.stack([same, other])
    far = {}
    for step in (1, -1):
        for hops in (1, 2):
            pair = lax.ppermute(near[step], "tp", ring_pairs(z_count, step * hops))
            arrays.append(pair)
            origins += [(-step * (hops + 1) % z_count, 0), (-step * (hops + 1) % z_count, 1)]
            far[step, hops] = pair
    last = lax.ppermute(far[1, 2], "tp", ring_pairs(z_count, 1))
    arrays.append(last)
    origins += [(-4 % z_count, 0), (-4 % z_count, 1)]
    table = [[0] * Y_LO for _ in range(z_count)]
    for index, (dz, dy) in enumerate(origins):
        table[dz][dy] = index
    feat_width = tp_count * own_width
    hid_blocks = FF // tp_count // tile
    share = own_rows // tp_count
    outgoing = ffn(counts, gu_blocks, down_blocks, me.astype(jnp.int32),
                   jnp.array(table, jnp.int32).reshape(-1), arrays, gate_tiles, up_tiles,
                   down_tiles, hid_blocks, ctx_count, share)
    incoming = lax.all_to_all(
        outgoing.reshape(ctx_count * tp_count, share, feat_width // ctx_count),
        ("ctx", "tp"), 0, 0, tiled=True,
    )
    total = jnp.sum(
        incoming.reshape(ctx_count, tp_count, share, -1).astype(jnp.float32), axis=1
    )
    return jnp.transpose(total, (1, 0, 2)).astype(jnp.bfloat16)


def solution(mesh):
    return jax.shard_map(
        per_device,
        mesh=mesh,
        in_specs=(
            P("ctx", "tp"),
            P("tp", None, None),
            P("tp", None, None),
            P("tp", None, None),
            P(None, "tp"),
            P(None, "tp"),
            P(None, "tp"),
        ),
        out_specs=P("tp", None, "ctx"),
        check_vma=False,
    )
```

```python
import functools

import jax
import jax.numpy as jnp
from jax import lax
from jax.experimental import pallas as pl
from jax.experimental.pallas import tpu as pltpu
from jax.sharding import PartitionSpec as P

FF = 16384
Y_LO = 2
CHUNKS = 2


def ffn_kernel(layout, cnt_ref, gu_ref, dn_ref, me_ref, table_ref, *refs):
    n_src = len(layout)
    n_ops = len(refs) - 12
    piece_refs = refs[:n_ops]
    (g_hbm, u_hbm, d_hbm, out_ref, normed_s, accg_s, accu_s, hid_s, acco_s, gu_v, d_v,
     sems) = refs[n_ops:]
    rows, width = piece_refs[0].shape

    def piece(s, cols):
        ref = piece_refs[layout[s][0]]
        return ref[:, cols] if layout[s][1] < 0 else ref[layout[s][1], :, cols]

    tile = g_hbm.shape[1]
    slots = g_hbm.shape[0]
    step = slots // CHUNKS
    copies = []
    for k in range(CHUNKS):
        part = pl.ds(k * step, step)
        copies.append((
            pltpu.make_async_copy(g_hbm.at[part], gu_v.at[part, :, 0:tile], sems.at[0, k]),
            pltpu.make_async_copy(u_hbm.at[part], gu_v.at[part, :, tile:2 * tile], sems.at[1, k]),
        ))
    down_copies = [
        pltpu.make_async_copy(d_hbm.at[pl.ds(k * step, step)], d_v.at[pl.ds(k * step, step)],
                              sems.at[2, k])
        for k in range(CHUNKS)
    ]
    for gate_copy, up_copy in copies:
        gate_copy.start()
        up_copy.start()
    for down_copy in down_copies:
        down_copy.start()
    per_src = width // tile
    feat = n_src * width
    ss = jnp.zeros((rows, 1), jnp.float32)
    for s in range(n_src):
        x = piece(s, slice(None)).astype(jnp.float32)
        ss = ss + jnp.sum(x * x, axis=1, keepdims=True)
    scale = lax.rsqrt(ss / feat + 1e-05)
    for s in range(n_src):
        for h in range(per_src):
            x = piece(s, slice(h * tile, (h + 1) * tile)).astype(jnp.float32)
            normed_s[s * per_src + h] = (x * scale).astype(jnp.bfloat16)
    accg_s[...] = jnp.zeros(accg_s.shape, jnp.float32)
    accu_s[...] = jnp.zeros(accu_s.shape, jnp.float32)

    z_count = n_src // Y_LO
    my_z = me_ref[0] // Y_LO
    my_y = me_ref[0] % Y_LO

    def gu_body(m, carry):
        in_tile = gu_ref[0, m]
        source = in_tile // per_src
        dz = (source // Y_LO - my_z + z_count) % z_count
        dy = jnp.where(source % Y_LO == my_y, 0, 1)
        x = normed_s[table_ref[dz * Y_LO + dy] * per_src + in_tile % per_src]
        h = gu_ref[1, m]
        live = (m < cnt_ref[0]).astype(jnp.float32)
        both = jnp.dot(x, gu_v[m], preferred_element_type=jnp.float32) * live
        accg_s[h] += both[:, :tile]
        accu_s[h] += both[:, tile:]
        return carry

    for k, (gate_copy, up_copy) in enumerate(copies):
        gate_copy.wait()
        up_copy.wait()
        lax.fori_loop(k * step, (k + 1) * step, gu_body, 0, unroll=True)
    g = accg_s[...]
    hid_s[...] = (g * jax.nn.sigmoid(g) * accu_s[...]).astype(jnp.bfloat16)
    acco_s[...] = jnp.zeros(acco_s.shape, jnp.float32)

    def dn_body(m, carry):
        o = dn_ref[1, m]
        live = (m < cnt_ref[1]).astype(jnp.float32)
        acco_s[o] += jnp.dot(hid_s[dn_ref[0, m]], d_v[m], preferred_element_type=jnp.float32) * live
        return carry

    for k, down_copy in enumerate(down_copies):
        down_copy.wait()
        lax.fori_loop(k * step, (k + 1) * step, dn_body, 0, unroll=True)
    groups, dests, share, group_width = out_ref.shape
    for h in range(per_src):
        acco_s[me_ref[0] * per_src + h] += piece(0, slice(h * tile, (h + 1) * tile)).astype(jnp.float32)
    per_group = group_width // tile
    for o in range(acco_s.shape[0]):
        block = acco_s[o].reshape(dests, share, tile).astype(out_ref.dtype)
        group, half = divmod(o, per_group)
        out_ref[group, :, :, half * tile:(half + 1) * tile] = block


def ffn(counts, gu_blocks, down_blocks, me, table, pieces, gate_tiles, up_tiles, down_tiles,
        hid_blocks, groups, share):
    layout = []
    for index, array in enumerate(pieces):
        layout += [(index, -1)] if array.ndim == 2 else [(index, sub) for sub in range(array.shape[0])]
    n_src = len(layout)
    rows, width = pieces[0].shape
    tile = gate_tiles.shape[1]
    in_blocks = n_src * width // tile
    smem = pl.BlockSpec(memory_space=pltpu.SMEM)
    vmem = pl.BlockSpec(memory_space=pltpu.VMEM)
    hbm = pl.BlockSpec(memory_space=pl.ANY)
    slots = gate_tiles.shape[0]
    return pl.pallas_call(
        functools.partial(ffn_kernel, tuple(layout)),
        out_shape=jax.ShapeDtypeStruct((groups, rows // share, share, in_blocks * tile // groups),
                                       jnp.bfloat16),
        in_specs=[smem] * 5 + [vmem] * len(pieces) + [hbm] * 3,
        out_specs=vmem,
        scratch_shapes=[
            pltpu.VMEM((in_blocks, rows, tile), jnp.bfloat16),
            pltpu.VMEM((hid_blocks, rows, tile), jnp.float32),
            pltpu.VMEM((hid_blocks, rows, tile), jnp.float32),
            pltpu.VMEM((hid_blocks, rows, tile), jnp.bfloat16),
            pltpu.VMEM((in_blocks, rows, tile), jnp.float32),
            pltpu.VMEM((slots, tile, 2 * tile), jnp.bfloat16),
            pltpu.VMEM((slots, tile, tile), jnp.bfloat16),
            pltpu.SemaphoreType.DMA((3, CHUNKS)),
        ],
    )(counts.reshape(-1), gu_blocks, down_blocks, me.reshape(1), table, *pieces, gate_tiles,
      up_tiles, down_tiles)

def ring_pairs(count, step, flip=0):
    return [(i, ((i // Y_LO + step) % count) * Y_LO + (i % Y_LO ^ flip)) for i in range(count * Y_LO)]


def per_device(tokens, gate_tiles, up_tiles, down_tiles, gu_blocks, down_blocks, counts):
    tp_count = lax.axis_size("tp")
    ctx_count = lax.axis_size("ctx")
    z_count = tp_count // Y_LO
    own_rows, own_width = tokens.shape
    tile = gate_tiles.shape[1]
    per_src = own_width // tile
    me = lax.axis_index("tp")
    my_z = me // Y_LO
    my_y = me % Y_LO
    swap = [(i, i ^ 1) for i in range(tp_count)]
    arrays = [tokens, lax.ppermute(tokens, "tp", swap)]
    origins = [(0, 0), (0, 1)]
    near = {}
    for step in (1, -1):
        same = lax.ppermute(tokens, "tp", ring_pairs(z_count, step))
        other = lax.ppermute(tokens, "tp", ring_pairs(z_count, step, 1))
        arrays += [same, other]
        origins += [(-step % z_count, 0), (-step % z_count, 1)]
        near[step] = jnp.stack([same, other])
    far = {}
    for step in (1, -1):
        for hops in (1, 2):
            pair = lax.ppermute(near[step], "tp", ring_pairs(z_count, step * hops))
            arrays.append(pair)
            origins += [(-step * (hops + 1) % z_count, 0), (-step * (hops + 1) % z_count, 1)]
            far[step, hops] = pair
    last = lax.ppermute(far[1, 2], "tp", ring_pairs(z_count, 1))
    arrays.append(last)
    origins += [(-4 % z_count, 0), (-4 % z_count, 1)]
    table = [[0] * Y_LO for _ in range(z_count)]
    for index, (dz, dy) in enumerate(origins):
        table[dz][dy] = index
    feat_width = tp_count * own_width
    hid_blocks = FF // tp_count // tile
    share = own_rows // tp_count
    outgoing = ffn(counts, gu_blocks, down_blocks, me.astype(jnp.int32),
                   jnp.array(table, jnp.int32).reshape(-1), arrays, gate_tiles, up_tiles,
                   down_tiles, hid_blocks, ctx_count, share)
    incoming = lax.all_to_all(
        outgoing.reshape(ctx_count * tp_count, share, feat_width // ctx_count),
        ("ctx", "tp"), 0, 0, tiled=True,
    )
    total = jnp.sum(
        incoming.reshape(ctx_count, tp_count, share, -1).astype(jnp.float32), axis=1
    )
    return jnp.transpose(total, (1, 0, 2)).astype(jnp.bfloat16)


def solution(mesh):
    return jax.shard_map(
        per_device,
        mesh=mesh,
        in_specs=(
            P("ctx", "tp"),
            P("tp", None, None),
            P("tp", None, None),
            P("tp", None, None),
            P(None, "tp"),
            P(None, "tp"),
            P(None, "tp"),
        ),
        out_specs=P("tp", None, "ctx"),
        check_vma=False,
    )
```
